32 devices in a mesh: pulse: 16 (over z, x, core), range: 2 (over y).
Axes of the slice: x: 2, y: 2, z: 4, core: 2. Of those that a mesh axis runs over, the one named last changes fastest.
Arguments:
- echo: bfloat16 [32, 2, 32768], P('pulse', None, 'range'), may hold values from -6 to 6
- chirp_phase: float32 [256], replicated, may hold values from -0.5 to 201.5624
- rec_phase: float32 [2, 2048, 2], P('range', 'pulse'), may hold values from -3.140625 to 3.140625
- rec_start: int32 [2, 2048], P('range', 'pulse'), may hold values from 0 to 32256
- rec_owner: int32 [2, 2048, 1], P('range', 'pulse'), may hold values from 0 to 31; in each aligned block of 128 rows (0 to 127, 128 to 255, ..., all dimensions but the last counted through in order) at most 6 rows name the same one
- rec_row: int32 [2, 2048], P('range', 'pulse'), may hold values from 0 to 63
- rec_weight: float32 [2, 2048], P('range', 'pulse'), may hold values from 0.2 to 1
- rec_count: int32 [2, 16], P('range', 'pulse'), may hold values from 96 to 128, as said below
- prior: bfloat16 [512, 2, 1024], P('pulse', None, 'range'), may hold values from -6 to 6
- interp_weight: bfloat16 [64, 32], replicated, may hold values from -1 to 1
Outputs:
- tiles: float32 [1024, 2, 1024], P('pulse', None, 'range')
The draws below stay inside these ranges and needn't reach their ends.
Inputs may be any that keep to these rules, and one draw needn't show every extreme that they name: `rec_owner`: in each aligned block of 128 record slots (one device's slots) no owner is named more than 6 times. Owner o is the tile of pulse index o // 2 and range index o % 2, 2 being the number of range devices. `rec_count`: some subimage has all 128 slots live.
All inputs are finite; a program needn't handle non-finite values.
Results may differ from the reference program's by a relative error of at most 0.0034.
Values may be sent and summed in bfloat16 or wider, within the bound.
No kernel may reach another device: no remote copies, remote signals or barrier semaphores. Data moves between devices by JAX's collectives and lax.ppermute only.
A program may use at most 64 MiB of HBM per device.

```python
import math
import jax
import jax.numpy as jnp
import numpy as np
from jax import lax

RANGE = 32768
TAPS = 256
SEG = 512
PD = 2
REC = 128
OUT_ROWS = 64
PRIOR = 32
PULSES = 32
RECS = 2048
CAP = 6
N_PULSE = 16
N_RANGE = 2
DEVICES = 32


def draw_chirp_phase(key, part):
    rate_key, noise_key = jax.random.split(key)
    sweep_rate = jax.random.uniform(rate_key, (), jnp.float32, 0.6, 1.0)
    offset = jnp.arange(TAPS, dtype=jnp.float32) - TAPS / 2
    jitter = jax.random.uniform(noise_key, (TAPS,), jnp.float32, -0.5, 0.5)
    return math.pi * sweep_rate * offset * offset / TAPS + jitter


def draw_rec_count(key, part):
    count_key, row_key, col_key = jax.random.split(key, 3)
    counts = jax.random.randint(count_key, (N_RANGE, N_PULSE), 3 * REC // 4, REC + 1)
    row_pick = jax.random.randint(row_key, (), 0, N_RANGE)
    col_pick = jax.random.randint(col_key, (), 0, N_PULSE)
    return counts.at[row_pick, col_pick].set(REC)


def set_ends(array, key, least, largest):
    extent = array.shape
    spot = [jax.random.randint(jax.random.fold_in(key, axis), (), 0, extent[axis]) for axis in range(len(extent))]
    array = array.at[tuple(spot)].set(least)
    longest = extent.index(max(extent))
    spot[longest] = (spot[longest] + 1) % extent[longest]
    return array.at[tuple(spot)].set(largest)


def levels(key, shape, cuts, low, high):
    loudness, own = 1.0, jax.random.fold_in(key, 6)
    for position, parts in cuts:
        draws = jnp.exp(jax.random.uniform(jax.random.fold_in(own, position), (parts,), jnp.float32, low / len(cuts), high / len(cuts)))
        loudness = loudness * jnp.repeat(draws, shape[position] // parts).reshape([-1 if axis == position else 1 for axis in range(len(shape))])
    return loudness


def deal_out(own_key, own, number, rows, count, top, bound, lean):
    order = jax.random.permutation(own_key, count)
    packed, common = portions_of(count, rows * top, bound, lean, True), portions_of(count, rows * top, bound, lean, False)
    places = jnp.arange(count)

    def named(sizes, turn):
        used = int((sizes > 0).sum())
        fixed = max(1, used // 4)
        shifted = fixed + (places - fixed + turn * (used - fixed)) % max(1, count - fixed)
        return jnp.zeros((count,), jnp.int32).at[order[jnp.where(places < fixed, places, shifted)]].set(jnp.asarray(sizes, jnp.int32))

    sizes = jnp.where(number % 4 == 0, named(packed, number // 4), named(common, number - number // 4 - 1))
    mixed = jax.random.permutation(jax.random.fold_in(own, 3), count)
    source_of, taker = mixed[0:count // 2 * 2:2], mixed[1:count // 2 * 2:2]
    room = jnp.minimum(sizes[source_of] - 1, bound - sizes[taker]) // 2
    room = jnp.where((source_of == order[0]) | (taker == order[0]) | (sizes[taker] == 0), 0, jnp.maximum(room, 0))
    shifted = jax.random.randint(jax.random.fold_in(own, 4), (count // 2,), 0, 1 << 20) % (room + 1)
    sizes = sizes.at[source_of].add(-shifted).at[taker].add(shifted)
    members = jnp.searchsorted(jnp.cumsum(sizes), jnp.arange(rows * top), side="right").astype(jnp.int32)
    grid = members.reshape(top, rows).T
    grid = grid[jax.random.permutation(jax.random.fold_in(own, 1), rows)]
    turn = jax.random.randint(jax.random.fold_in(own, 2), (rows, 1), 0, top)
    return jnp.take_along_axis(grid, (jnp.arange(top)[None, :] + turn) % top, axis=1)


def portions_of(count, total, bound, skew, full):
    portions = [(1 << 20) // math.isqrt(rank ** skew) + 1 for rank in range(1, count + 1)]
    largest = bound if full else min(bound, max(-(-total // count), total * portions[0] // sum(portions)))
    least = 1 if total - largest >= count - 1 else 0
    given, surplus = [largest] + [least] * (count - 1), total - largest - least * (count - 1)
    while surplus > 0:
        free = [i for i in range(1, count) if given[i] < largest] or [i for i in range(1, count) if given[i] < bound]
        pool, remaining = sum([portions[i] for i in free]), surplus
        for i in free:
            addition = min(bound - given[i], max(1, remaining * portions[i] // pool), surplus)
            given[i] = given[i] + addition
            surplus = surplus - addition
    return np.array(given)


def bell_draw(stream_key, dims, deviation, limit, shards=(), held_as=jnp.bfloat16):
    array = jax.random.normal(stream_key, dims, jnp.float32) * deviation
    if len(shards) > 0:
        array = levels(stream_key, dims, shards, -0.22, 0.18) * array
    return jnp.clip(array, min=-limit, max=limit).astype(held_as)


def setup_inputs(seed: int = 0) -> dict:
    seeds = jax.random.split(jax.random.key(seed), 11)
    echo = bell_draw(seeds[0], (PULSES, 2, RANGE), 1.0, 6.0, ((0, 16), (2, 2)))
    chirp_phase = draw_chirp_phase(jax.random.fold_in(seeds[10], 71), 0)
    rec_phase = jnp.clip(jax.random.uniform(seeds[2], (N_RANGE, RECS, PD), jnp.float32, -3.140625, 3.140625), -3.140625, 3.140625)
    rec_start = set_ends(jax.random.randint(seeds[3], (N_RANGE, RECS), 0, RANGE - SEG + 1), jax.random.fold_in(seeds[3], 1), 0, RANGE - SEG).astype(jnp.int32)
    rec_owner_keys = jax.random.split(jax.random.fold_in(seeds[4], 1), N_RANGE * RECS // REC)
    rec_owner_turns = jax.random.permutation(jax.random.fold_in(seeds[4], 3), N_RANGE * RECS // REC)
    rec_owner = jax.vmap(lambda own, number: deal_out(jax.random.fold_in(seeds[4], 2), own, number, REC, DEVICES, 1, CAP, 2))(rec_owner_keys, rec_owner_turns).reshape((N_RANGE, RECS, 1))
    rec_row = set_ends(jax.random.randint(seeds[5], (N_RANGE, RECS), 0, OUT_ROWS), jax.random.fold_in(seeds[5], 1), 0, OUT_ROWS - 1).astype(jnp.int32)
    rec_weight = jnp.clip(0.2 + 0.8 * jax.random.uniform(seeds[6], (N_RANGE, RECS), jnp.float32) ** levels(seeds[6], (N_RANGE, RECS), ((0, 2), (1, 16)), -0.2, 0.2), 0.2, 1.0)
    rec_count = draw_rec_count(jax.random.fold_in(seeds[10], 71), 0)
    prior = bell_draw(seeds[8], (N_PULSE * PRIOR, 2, N_RANGE * SEG), 1.0, 6.0, ((0, 16), (2, 2)))
    interp_weight = bell_draw(seeds[9], (OUT_ROWS, PRIOR), PRIOR ** -0.5, 1.0)
    return dict(echo=echo, chirp_phase=chirp_phase, rec_phase=rec_phase, rec_start=rec_start, rec_owner=rec_owner, rec_row=rec_row, rec_weight=rec_weight, rec_count=rec_count, prior=prior, interp_weight=interp_weight)


def chirp_matrix(chirp_phase):
    tap_count = chirp_phase.shape[0]
    tap_scale = 1.0 / jnp.sqrt(jnp.float32(tap_count))
    real_taps = jnp.cos(chirp_phase) * tap_scale
    imag_taps = jnp.sin(chirp_phase) * tap_scale

    def banded(values):
        padded = jnp.concatenate([values, jnp.zeros((tap_count + 1,), jnp.float32)])
        return jnp.tile(padded, tap_count)[:2 * tap_count * tap_count].reshape(tap_count, 2 * tap_count).T
    real_band = banded(real_taps)
    imag_band = banded(imag_taps)
    upper = jnp.concatenate([real_band, -imag_band], axis=1)
    lower = jnp.concatenate([imag_band, real_band], axis=1)
    return jnp.concatenate([upper, lower], axis=0).astype(jnp.bfloat16)

def compress(echo_block, tail_rim, filter_matrix):
    pulses, planes, bin_count = echo_block.shape
    tap_count = filter_matrix.shape[1] // 2
    block_count = bin_count // tap_count
    extended = jnp.concatenate([echo_block, tail_rim], axis=2)
    left_half = extended[:, :, :bin_count].reshape(pulses, planes, block_count, tap_count)
    right_half = extended[:, :, tap_count:].reshape(pulses, planes, block_count, tap_count)
    windows = jnp.concatenate([left_half, right_half], axis=3)
    windows = windows.transpose(0, 2, 1, 3).reshape(pulses * block_count, 2 * planes * tap_count)
    filtered = jnp.dot(windows, filter_matrix, preferred_element_type=jnp.float32)
    filtered = filtered.reshape(pulses, block_count, planes, tap_count).transpose(0, 2, 1, 3)
    return filtered.reshape(pulses, planes, bin_count).astype(jnp.bfloat16)

def form_records(profiles, starts, phases, scales):

    def window_at(start):
        return lax.dynamic_slice_in_dim(profiles, start, SEG, 2)
    windows = jax.vmap(window_at)(starts).astype(jnp.float32)
    cosine = jnp.cos(phases).astype(jnp.bfloat16).astype(jnp.float32)
    sine_part = jnp.sin(phases).astype(jnp.bfloat16).astype(jnp.float32)
    real_part = windows[:, :, 0]
    imag_part = windows[:, :, 1]
    out_real = jnp.einsum('bk,bks->bs', cosine, real_part) - jnp.einsum('bk,bks->bs', sine_part, imag_part)
    out_imag = jnp.einsum('bk,bks->bs', cosine, imag_part) + jnp.einsum('bk,bks->bs', sine_part, real_part)
    return jnp.stack([out_real, out_imag], axis=1) * scales[:, None, None]

def reference(echo, chirp_phase, rec_phase, rec_start, rec_owner, rec_row, rec_weight, rec_count, prior, interp_weight):
    filter_matrix = chirp_matrix(chirp_phase)
    grouped = echo.reshape(N_PULSE, PD, 2, RANGE)
    empty_rim = jnp.zeros((PD, 2, TAPS), echo.dtype)
    compressed = lax.map(lambda group: compress(group, empty_rim, filter_matrix), grouped)

    def by_pulse(values):
        shaped = values.reshape((N_RANGE, N_PULSE, REC) + values.shape[2:])
        order = (1, 0, 2) + tuple(range(3, shaped.ndim))
        return shaped.transpose(order).reshape((N_PULSE, N_RANGE * REC) + values.shape[2:])
    starts = by_pulse(rec_start).astype(jnp.int32)
    phases = by_pulse(rec_phase)
    owners = by_pulse(rec_owner[:, :, 0]).astype(jnp.int32)
    dest_rows = by_pulse(rec_row).astype(jnp.int32)
    live_mask = (jnp.arange(REC)[None, None, :] < rec_count[:, :, None]).astype(jnp.float32)
    scales = live_mask * rec_weight.reshape(N_RANGE, N_PULSE, REC) / jnp.sqrt(jnp.float32(PD))
    scales = scales.transpose(1, 0, 2).reshape(N_PULSE, N_RANGE * REC)
    targets = ((owners // N_RANGE * OUT_ROWS + dest_rows) * N_RANGE + owners % N_RANGE).astype(jnp.int32)
    initial = jnp.zeros((N_PULSE * OUT_ROWS * N_RANGE, 2, SEG), jnp.float32)

    def add_subimage(total, items):
        profiles, start_list, phase_list, scale_list, target_list = items
        records = form_records(profiles, start_list, phase_list, scale_list)
        rounded = lax.optimization_barrier(records.astype(jnp.bfloat16))
        return (total.at[target_list].add(rounded.astype(jnp.float32)), None)
    total, _ = lax.scan(add_subimage, initial, (compressed, starts, phases, scales, targets))
    total = total.reshape(N_PULSE * OUT_ROWS, N_RANGE, 2, SEG).transpose(0, 2, 1, 3)
    total = total.reshape(N_PULSE * OUT_ROWS, 2, N_RANGE * SEG)
    coarse = prior.astype(jnp.float32).reshape(N_PULSE, PRIOR, 2 * N_RANGE * SEG)
    fine = jnp.einsum('rm,qmx->qrx', interp_weight.astype(jnp.float32), coarse, precision=lax.Precision.HIGHEST)
    fine = fine.reshape(N_PULSE * OUT_ROWS, 2, N_RANGE * SEG)
    return fine + total
```

```python
import jax
import jax.numpy as jnp
from jax import lax
from jax.experimental import pallas as pl
from jax.experimental.pallas import tpu as pltpu
from jax.sharding import PartitionSpec as P

SEG = 512
LANE = 128
GROUP = 8
SPAN = SEG + LANE


def chirp_matrix(chirp_phase):
    tap_count = chirp_phase.shape[0]
    tap_scale = 1.0 / jnp.sqrt(jnp.float32(tap_count))
    real_taps = jnp.cos(chirp_phase) * tap_scale
    imag_taps = jnp.sin(chirp_phase) * tap_scale

    def banded(values):
        padded = jnp.concatenate([values, jnp.zeros((tap_count + 1,), jnp.float32)])
        return (
            jnp.tile(padded, tap_count)[: 2 * tap_count * tap_count]
            .reshape(tap_count, 2 * tap_count)
            .T
        )

    real_band = banded(real_taps)
    imag_band = banded(imag_taps)
    upper = jnp.concatenate([real_band, -imag_band], axis=1)
    lower = jnp.concatenate([imag_band, real_band], axis=1)
    return jnp.concatenate([upper, lower], axis=0).astype(jnp.bfloat16)


def compress(echo_block, tail_rim, filter_matrix):
    pulses, planes, bin_count = echo_block.shape
    tap_count = filter_matrix.shape[1] // 2
    block_count = bin_count // tap_count
    extended = jnp.concatenate([echo_block, tail_rim], axis=2)
    left_half = extended[:, :, :bin_count].reshape(pulses, planes, block_count, tap_count)
    right_half = extended[:, :, tap_count:].reshape(pulses, planes, block_count, tap_count)
    windows = jnp.concatenate([left_half, right_half], axis=3)
    windows = windows.transpose(0, 2, 1, 3).reshape(pulses * block_count, 2 * planes * tap_count)
    filtered = jnp.dot(windows, filter_matrix, preferred_element_type=jnp.float32)
    filtered = filtered.reshape(pulses, block_count, planes, tap_count).transpose(0, 2, 1, 3)
    return filtered.reshape(pulses, planes, bin_count).astype(jnp.bfloat16)


def records_kernel(starts_ref, prof_ref, coef_ref, off_ref, out_ref, buf):
    bins = prof_ref.shape[1]
    last_base = bins - SPAN
    groups = out_ref.shape[0] // GROUP

    def group(g, carry):
        for r in range(GROUP):
            st = starts_ref[g * GROUP + r]
            base = pl.multiple_of(jnp.minimum((st // LANE) * LANE, last_base), LANE)
            for kp in range(4):
                buf[kp, pl.ds(r, 1), :] = prof_ref[pl.ds(kp, 1), pl.ds(base, SPAN)]
        rows = pl.ds(pl.multiple_of(g * GROUP, GROUP), GROUP)
        coef = coef_ref[rows, :]
        c0, s0, c1, s1, sc = (coef[:, i : i + 1] for i in range(5))
        re0, im0, re1, im1 = buf[0], buf[1], buf[2], buf[3]
        out_re = ((c0 * re0 + c1 * re1) - (s0 * im0 + s1 * im1)) * sc
        out_im = ((c0 * im0 + c1 * im1) + (s0 * re0 + s1 * re1)) * sc
        off = off_ref[rows, :][:, 0:1]
        for bit in range(8):
            step = 1 << bit
            chosen = ((off >> bit) & 1) == 1
            out_re = jnp.where(chosen, pltpu.roll(out_re, SPAN - step, 1), out_re)
            out_im = jnp.where(chosen, pltpu.roll(out_im, SPAN - step, 1), out_im)
        out_ref[rows, 0:SEG] = out_re[:, :SEG].astype(out_ref.dtype)
        out_ref[rows, SEG : 2 * SEG] = out_im[:, :SEG].astype(out_ref.dtype)
        return carry

    lax.fori_loop(0, groups, group, 0)


def form_records(prof4, starts, coef, offs):
    slots = starts.shape[0]
    vmem = pl.BlockSpec(memory_space=pltpu.VMEM)
    return pl.pallas_call(
        records_kernel,
        out_shape=jax.ShapeDtypeStruct((slots, 2 * SEG), jnp.bfloat16),
        in_specs=[pl.BlockSpec(memory_space=pltpu.SMEM), vmem, vmem, vmem],
        out_specs=vmem,
        scratch_shapes=[pltpu.VMEM((4, GROUP, SPAN), jnp.float32)],
    )(starts, prof4, coef, offs)


def on_device(
    echo,
    chirp_phase,
    rec_phase,
    rec_start,
    rec_owner,
    rec_row,
    rec_weight,
    rec_count,
    prior,
    interp_weight,
):
    pulse_count = lax.axis_size("pulse")
    range_count = lax.axis_size("range")
    owner_total = pulse_count * range_count
    axes = ("pulse", "range")
    me = lax.axis_index("pulse") * range_count + lax.axis_index("range")

    slot_count = rec_start.shape[1]
    owners = rec_owner[0, :, 0]
    dest_rows = rec_row[0]
    out_rows = interp_weight.shape[0]
    capacity = max(2, 3 * slot_count // (2 * owner_total))

    codes = owners * out_rows + dest_rows
    all_codes = lax.all_gather(codes, axes, axis=0, tiled=False)

    filter_matrix = chirp_matrix(chirp_phase)
    tap_count = chirp_phase.shape[0]
    raw_echo = lax.all_gather(echo, "range", axis=2, tiled=True)
    profiles = compress(raw_echo, jnp.zeros_like(raw_echo[:, :, :tap_count]), filter_matrix)
    pulses, planes, bin_total = profiles.shape
    prof4 = profiles.reshape(pulses * planes, bin_total).astype(jnp.float32)

    starts = rec_start[0]
    phases = rec_phase[0]
    weights = rec_weight[0]
    live_mask = (jnp.arange(slot_count) < rec_count[0, 0]).astype(jnp.float32)
    scales = live_mask * weights / jnp.sqrt(jnp.float32(pulses))
    cosine = jnp.cos(phases).astype(jnp.bfloat16).astype(jnp.float32)
    sine_part = jnp.sin(phases).astype(jnp.bfloat16).astype(jnp.float32)
    coef = jnp.stack(
        [cosine[:, 0], sine_part[:, 0], cosine[:, 1], sine_part[:, 1], scales]
        + [jnp.zeros_like(scales)] * 3,
        axis=1,
    )
    base = jnp.minimum(starts // LANE * LANE, bin_total - SPAN)
    offs = jnp.broadcast_to((starts - base)[:, None], (slot_count, LANE)).astype(jnp.int32)
    records = form_records(prof4, starts, coef, offs)

    owner_marks = (owners[:, None] == jnp.arange(owner_total)[None, :]).astype(jnp.int32)
    earlier = jnp.cumsum(owner_marks, axis=0) - owner_marks
    slot_rank = jnp.sum(earlier * owner_marks, axis=1)
    slot_index = owners * capacity + slot_rank
    placement = slot_index[None, :] == jnp.arange(owner_total * capacity)[:, None]
    outgoing = jnp.dot(
        placement.astype(jnp.bfloat16), records, preferred_element_type=jnp.float32
    ).astype(jnp.bfloat16)
    incoming = lax.all_to_all(outgoing, axes, 0, 0, tiled=True)

    mine = (all_codes // out_rows == me).astype(jnp.int32)
    rank = jnp.cumsum(mine, axis=1) - mine
    row_of = all_codes % out_rows
    picks = (mine[:, None, :] == 1) & (rank[:, None, :] == jnp.arange(capacity)[None, :, None])
    slot_rows = jnp.sum(jnp.where(picks, row_of[:, None, :], 0), axis=2).reshape(-1)
    row_table = (slot_rows[None, :] == jnp.arange(out_rows)[:, None]).astype(jnp.bfloat16)

    prior_rows = prior.shape[0]
    fine = jnp.dot(
        interp_weight, prior.reshape(prior_rows, -1), preferred_element_type=jnp.float32
    )
    merged = fine + jnp.dot(row_table, incoming, preferred_element_type=jnp.float32)
    return merged.reshape(out_rows, planes, -1)


def solution(mesh):
    placed = (
        P("pulse", None, "range"),
        P(),
        P("range", "pulse", None),
        P("range", "pulse"),
        P("range", "pulse", None),
        P("range", "pulse"),
        P("range", "pulse"),
        P("range", "pulse"),
        P("pulse", None, "range"),
        P(),
    )
    return jax.shard_map(
        on_device, mesh=mesh, in_specs=placed, out_specs=P("pulse", None, "range"), check_vma=False
    )
```

```python
import jax
import jax.numpy as jnp
from jax import lax
from jax.experimental import pallas as pl
from jax.experimental.pallas import tpu as pltpu
from jax.sharding import PartitionSpec as P

SEG = 512
LANE = 128
GROUP = 8


def chirp_matrix(chirp_phase):
    tap_count = chirp_phase.shape[0]
    tap_scale = 1.0 / jnp.sqrt(jnp.float32(tap_count))
    real_taps = jnp.cos(chirp_phase) * tap_scale
    imag_taps = jnp.sin(chirp_phase) * tap_scale

    def banded(values):
        padded = jnp.concatenate([values, jnp.zeros((tap_count + 1,), jnp.float32)])
        return (
            jnp.tile(padded, tap_count)[: 2 * tap_count * tap_count]
            .reshape(tap_count, 2 * tap_count)
            .T
        )

    real_band = banded(real_taps)[: tap_count + LANE, :LANE]
    imag_band = banded(imag_taps)[: tap_count + LANE, :LANE]
    upper = jnp.concatenate([real_band, -imag_band], axis=1)
    lower = jnp.concatenate([imag_band, real_band], axis=1)
    return jnp.concatenate([upper, lower], axis=0).astype(jnp.bfloat16)


def compress_chunks(echo_full, filter_matrix, chunk_total):
    pulses, planes, bin_count = echo_full.shape
    taps = filter_matrix.shape[0] // planes - LANE
    reach = taps // LANE
    padded = jnp.pad(
        echo_full, ((0, 0), (0, 0), (0, (chunk_total + reach) * LANE - bin_count))
    )
    chunks = padded.reshape(pulses, planes, chunk_total + reach, LANE)
    windows = jnp.concatenate(
        [chunks[:, :, lead : lead + chunk_total] for lead in range(reach + 1)], axis=3
    )
    windows = windows.transpose(0, 2, 1, 3).reshape(pulses * chunk_total, -1)
    filtered = jnp.dot(windows, filter_matrix, preferred_element_type=jnp.float32)
    filtered = lax.reduce_precision(filtered, 8, 7)
    return filtered.reshape(pulses, chunk_total, planes * LANE)


def records_kernel(starts_ref, slot_ref, coef_ref, prof_ref, info_ref, out_ref):
    slots = starts_ref.shape[0]
    owners = info_ref.shape[0]
    per_owner = out_ref.shape[0] // owners
    lane_ids = lax.broadcasted_iota(jnp.int32, (GROUP, LANE), 1)
    row_ids = lax.broadcasted_iota(jnp.int32, (GROUP, LANE), 0)
    out_ref[...] = jnp.zeros(out_ref.shape, out_ref.dtype)

    def put_info(o, carry):
        out_ref[o * per_owner + per_owner - 1] = info_ref[o]
        return carry

    lax.fori_loop(0, owners, put_info, 0)

    def record(j, carry):
        st = starts_ref[j]
        first = st // LANE
        off = st - first * LANE
        aligned = pl.multiple_of((first // GROUP) * GROUP, GROUP)
        lift = (2 * GROUP - (first - aligned)) % (2 * GROUP)
        parts = []
        for k in range(2):
            rows = prof_ref[k, pl.ds(aligned, 2 * GROUP), :]
            rows = pltpu.roll(rows, lift, 0)[:GROUP]
            parts.append((rows[:, :LANE], rows[:, LANE:]))
        (re0, im0), (re1, im1) = parts
        c0, s0, c1, s1, sc = (coef_ref[i, j] for i in range(5))
        out_re = ((c0 * re0 + c1 * re1) - (s0 * im0 + s1 * im1)) * sc
        out_im = ((c0 * im0 + c1 * im1) + (s0 * re0 + s1 * re1)) * sc
        turn = (LANE - off) % LANE
        keep = lane_ids < LANE - off
        shifted = []
        for z in (out_re, out_im):
            rot = pltpu.roll(z, turn, 1)
            shifted.append(jnp.where(keep, rot, pltpu.roll(rot, GROUP - 1, 0)))
        tile = jnp.where(
            row_ids < GROUP // 2, shifted[0], pltpu.roll(shifted[1], GROUP // 2, 0)
        )
        out_ref[slot_ref[j]] = tile.astype(out_ref.dtype)
        return carry

    lax.fori_loop(0, slots, record, 0, unroll=8)


def form_payload(prof, starts, slot_index, coef, info, slot_total):
    vmem = pl.BlockSpec(memory_space=pltpu.VMEM)
    smem = pl.BlockSpec(memory_space=pltpu.SMEM)
    return pl.pallas_call(
        records_kernel,
        out_shape=jax.ShapeDtypeStruct((slot_total, GROUP, LANE), jnp.bfloat16),
        in_specs=[smem, smem, smem, vmem, vmem],
        out_specs=vmem,
    )(starts, slot_index, coef, prof, info)


def on_device(
    echo,
    chirp_phase,
    rec_phase,
    rec_start,
    rec_owner,
    rec_row,
    rec_weight,
    rec_count,
    prior,
    interp_weight,
):
    pulse_count = lax.axis_size("pulse")
    range_count = lax.axis_size("range")
    owner_total = pulse_count * range_count
    axes = ("pulse", "range")

    slot_count = rec_start.shape[1]
    owners = rec_owner[0, :, 0]
    dest_rows = rec_row[0]
    out_rows = interp_weight.shape[0]
    capacity = max(2, 3 * slot_count // (2 * owner_total))
    per_owner = capacity + 1
    slot_total = owner_total * per_owner

    filter_matrix = chirp_matrix(chirp_phase)
    if range_count == 2:
        other = lax.ppermute(echo, "range", [(0, 1), (1, 0)])
        first = lax.axis_index("range") == 0
        raw_echo = jnp.where(
            first, jnp.concatenate([echo, other], axis=2), jnp.concatenate([other, echo], axis=2)
        )
    else:
        raw_echo = lax.all_gather(echo, "range", axis=2, tiled=True)
    pulses, planes, bin_total = raw_echo.shape
    chunk_total = bin_total // LANE + 2 * GROUP
    prof = compress_chunks(raw_echo, filter_matrix, chunk_total)

    starts = rec_start[0]
    phases = rec_phase[0]
    weights = rec_weight[0]
    live_mask = (jnp.arange(slot_count) < rec_count[0, 0]).astype(jnp.float32)
    scales = live_mask * weights / jnp.sqrt(jnp.float32(pulses))
    cosine = lax.reduce_precision(jnp.cos(phases), 8, 7)
    sine_part = lax.reduce_precision(jnp.sin(phases), 8, 7)
    coef = jnp.stack([cosine[:, 0], sine_part[:, 0], cosine[:, 1], sine_part[:, 1], scales])

    owner_marks = (owners[:, None] == jnp.arange(owner_total)[None, :]).astype(jnp.int32)
    earlier = jnp.cumsum(owner_marks, axis=0) - owner_marks
    slot_rank = jnp.sum(earlier * owner_marks, axis=1)
    slot_index = owners * per_owner + jnp.minimum(slot_rank, capacity - 1)
    slot_index = jnp.clip(slot_index, 0, slot_total - 1).astype(jnp.int32)
    info_pos = slot_rank * out_rows + dest_rows
    info = jnp.dot(
        owner_marks.T.astype(jnp.bfloat16),
        (info_pos[:, None] == jnp.arange(GROUP * LANE)[None, :]).astype(jnp.bfloat16),
        preferred_element_type=jnp.float32,
    ).astype(jnp.bfloat16)
    info = info.reshape(owner_total, GROUP, LANE)

    outgoing = form_payload(prof, starts, slot_index, coef, info, slot_total)
    incoming = lax.all_to_all(
        outgoing.reshape(owner_total, per_owner, GROUP, LANE), axes, 0, 0, tiled=True
    )
    data = incoming[:, :capacity]
    row_table = incoming[:, capacity].reshape(owner_total, GROUP * LANE)[
        :, : capacity * out_rows
    ].reshape(owner_total, capacity, out_rows)
    gathered = jnp.einsum(
        "dkr,dkql->rql", row_table, data, preferred_element_type=jnp.float32
    )
    gathered = gathered.reshape(out_rows, planes, -1)
    fine = jnp.einsum(
        "rm,mps->rps", interp_weight, prior, preferred_element_type=jnp.float32
    )
    return fine + gathered


def solution(mesh):
    placed = (
        P("pulse", None, "range"),
        P(),
        P("range", "pulse", None),
        P("range", "pulse"),
        P("range", "pulse", None),
        P("range", "pulse"),
        P("range", "pulse"),
        P("range", "pulse"),
        P("pulse", None, "range"),
        P(),
    )
    return jax.shard_map(
        on_device, mesh=mesh, in_specs=placed, out_specs=P("pulse", None, "range"), check_vma=False
    )
```

```python
import jax
import jax.numpy as jnp
from jax import lax
from jax.experimental import pallas as pl
from jax.experimental.pallas import tpu as pltpu
from jax.sharding import PartitionSpec as P

SEG = 512
LANE = 128
GROUP = 8


def chirp_kernel(phase_ref, out_ref):
    taps = phase_ref.shape[1]
    rows = out_ref.shape[0] // 2
    span = out_ref.shape[1] // 2
    phase = phase_ref[...]
    scale = 1.0 / jnp.sqrt(jnp.float32(taps))
    bands = []
    for wave in (jnp.cos(phase) * scale, jnp.sin(phase) * scale):
        row = jnp.concatenate([wave, jnp.zeros((1, span - taps), jnp.float32)], axis=1)
        spread = jnp.broadcast_to(row, (rows, span))
        bands.append(pltpu.roll(spread, 0, 1, stride=1, stride_axis=0))
    real_band, imag_band = bands
    out_ref[0:rows, 0:span] = real_band.astype(out_ref.dtype)
    out_ref[0:rows, span : 2 * span] = imag_band.astype(out_ref.dtype)
    out_ref[rows : 2 * rows, 0:span] = (-imag_band).astype(out_ref.dtype)
    out_ref[rows : 2 * rows, span : 2 * span] = real_band.astype(out_ref.dtype)


def chirp_matrix(chirp_phase):
    taps = chirp_phase.shape[0]
    vmem = pl.BlockSpec(memory_space=pltpu.VMEM)
    return pl.pallas_call(
        chirp_kernel,
        out_shape=jax.ShapeDtypeStruct((2 * LANE, 2 * (taps + LANE)), jnp.bfloat16),
        in_specs=[vmem],
        out_specs=vmem,
    )(chirp_phase.reshape(1, taps))


def compress_chunks(echo_full, filter_matrix, chunk_total):
    pulses, planes, bin_count = echo_full.shape
    taps = filter_matrix.shape[1] // planes - LANE
    reach = taps // LANE
    padded = jnp.pad(
        echo_full, ((0, 0), (0, 0), (0, (chunk_total + reach) * LANE - bin_count))
    )
    chunks = padded.reshape(pulses, planes, chunk_total + reach, LANE)
    windows = jnp.concatenate(
        [chunks[:, :, lead : lead + chunk_total] for lead in range(reach + 1)], axis=3
    )
    windows = windows.transpose(0, 2, 1, 3).reshape(pulses * chunk_total, -1)
    filtered = lax.dot_general(
        windows, filter_matrix, (((1,), (1,)), ((), ())), preferred_element_type=jnp.float32
    )
    filtered = lax.reduce_precision(filtered, 8, 7)
    return filtered.reshape(pulses, chunk_total, planes * LANE)


def records_kernel(starts_ref, slot_ref, coef_ref, prof_ref, info_ref, out_ref):
    slots = starts_ref.shape[0]
    owners = info_ref.shape[0]
    per_owner = out_ref.shape[0] // owners
    lane_ids = lax.broadcasted_iota(jnp.int32, (GROUP, LANE), 1)
    row_ids = lax.broadcasted_iota(jnp.int32, (GROUP, LANE), 0)
    out_ref[...] = jnp.zeros(out_ref.shape, out_ref.dtype)

    def put_info(o, carry):
        out_ref[o * per_owner + per_owner - 1] = info_ref[o]
        return carry

    lax.fori_loop(0, owners, put_info, 0)

    def record(j, carry):
        st = starts_ref[j]
        first = st // LANE
        off = st - first * LANE
        aligned = pl.multiple_of((first // GROUP) * GROUP, GROUP)
        lift = (2 * GROUP - (first - aligned)) % (2 * GROUP)
        parts = []
        for k in range(2):
            rows = prof_ref[k, pl.ds(aligned, 2 * GROUP), :]
            rows = pltpu.roll(rows, lift, 0)[:GROUP]
            parts.append((rows[:, :LANE], rows[:, LANE:]))
        (re0, im0), (re1, im1) = parts
        c0, s0, c1, s1, sc = (coef_ref[i, j] for i in range(5))
        out_re = ((c0 * re0 + c1 * re1) - (s0 * im0 + s1 * im1)) * sc
        out_im = ((c0 * im0 + c1 * im1) + (s0 * re0 + s1 * re1)) * sc
        turn = (LANE - off) % LANE
        keep = lane_ids < LANE - off
        shifted = []
        for z in (out_re, out_im):
            rot = pltpu.roll(z, turn, 1)
            shifted.append(jnp.where(keep, rot, pltpu.roll(rot, GROUP - 1, 0)))
        tile = jnp.where(
            row_ids < GROUP // 2, shifted[0], pltpu.roll(shifted[1], GROUP // 2, 0)
        )
        out_ref[slot_ref[j]] = tile.astype(out_ref.dtype)
        return carry

    lax.fori_loop(0, slots, record, 0, unroll=8)


def form_payload(prof, starts, slot_index, coef, info, slot_total):
    vmem = pl.BlockSpec(memory_space=pltpu.VMEM)
    smem = pl.BlockSpec(memory_space=pltpu.SMEM)
    return pl.pallas_call(
        records_kernel,
        out_shape=jax.ShapeDtypeStruct((slot_total, GROUP, LANE), jnp.bfloat16),
        in_specs=[smem, smem, smem, vmem, vmem],
        out_specs=vmem,
    )(starts, slot_index, coef, prof, info)


def on_device(
    echo,
    chirp_phase,
    rec_phase,
    rec_start,
    rec_owner,
    rec_row,
    rec_weight,
    rec_count,
    prior,
    interp_weight,
):
    pulse_count = lax.axis_size("pulse")
    range_count = lax.axis_size("range")
    owner_total = pulse_count * range_count
    axes = ("pulse", "range")

    slot_count = rec_start.shape[1]
    owners = rec_owner[0, :, 0]
    dest_rows = rec_row[0]
    out_rows = interp_weight.shape[0]
    capacity = max(2, 3 * slot_count // (2 * owner_total))
    per_owner = capacity + 1
    slot_total = owner_total * per_owner

    filter_matrix = chirp_matrix(chirp_phase)
    if range_count == 2:
        other = lax.ppermute(echo, "range", [(0, 1), (1, 0)])
        first = lax.axis_index("range") == 0
        raw_echo = jnp.where(
            first, jnp.concatenate([echo, other], axis=2), jnp.concatenate([other, echo], axis=2)
        )
    else:
        raw_echo = lax.all_gather(echo, "range", axis=2, tiled=True)
    pulses, planes, bin_total = raw_echo.shape
    chunk_total = bin_total // LANE + 2 * GROUP
    prof = compress_chunks(raw_echo, filter_matrix, chunk_total)

    starts = rec_start[0]
    phases = rec_phase[0]
    weights = rec_weight[0]
    live_mask = (jnp.arange(slot_count) < rec_count[0, 0]).astype(jnp.float32)
    scales = live_mask * weights / jnp.sqrt(jnp.float32(pulses))
    cosine = lax.reduce_precision(jnp.cos(phases), 8, 7)
    sine_part = lax.reduce_precision(jnp.sin(phases), 8, 7)
    coef = jnp.stack([cosine[:, 0], sine_part[:, 0], cosine[:, 1], sine_part[:, 1], scales])

    owner_marks = (owners[:, None] == jnp.arange(owner_total)[None, :]).astype(jnp.int32)
    earlier = jnp.cumsum(owner_marks, axis=0) - owner_marks
    slot_rank = jnp.sum(earlier * owner_marks, axis=1)
    slot_index = owners * per_owner + jnp.minimum(slot_rank, capacity - 1)
    slot_index = jnp.clip(slot_index, 0, slot_total - 1).astype(jnp.int32)
    info_pos = slot_rank * out_rows + dest_rows
    info = jnp.dot(
        owner_marks.T.astype(jnp.bfloat16),
        (info_pos[:, None] == jnp.arange(GROUP * LANE)[None, :]).astype(jnp.bfloat16),
        preferred_element_type=jnp.float32,
    ).astype(jnp.bfloat16)
    info = info.reshape(owner_total, GROUP, LANE)

    outgoing = form_payload(prof, starts, slot_index, coef, info, slot_total)
    incoming = lax.all_to_all(
        outgoing.reshape(owner_total, per_owner, GROUP, LANE), axes, 0, 0, tiled=True
    )
    data = incoming[:, :capacity]
    row_table = incoming[:, capacity].reshape(owner_total, GROUP * LANE)[
        :, : capacity * out_rows
    ].reshape(owner_total, capacity, out_rows)
    gathered = jnp.einsum(
        "dkr,dkql->rql", row_table, data, preferred_element_type=jnp.float32
    )
    gathered = gathered.reshape(out_rows, planes, -1)
    fine = jnp.einsum(
        "rm,mps->rps", interp_weight, prior, preferred_element_type=jnp.float32
    )
    return fine + gathered


def solution(mesh):
    placed = (
        P("pulse", None, "range"),
        P(),
        P("range", "pulse", None),
        P("range", "pulse"),
        P("range", "pulse", None),
        P("range", "pulse"),
        P("range", "pulse"),
        P("range", "pulse"),
        P("pulse", None, "range"),
        P(),
    )
    return jax.shard_map(
        on_device, mesh=mesh, in_specs=placed, out_specs=P("pulse", None, "range"), check_vma=False
    )
```

```python
import functools

import jax
import jax.numpy as jnp
from jax import lax
from jax.experimental import pallas as pl
from jax.experimental.pallas import tpu as pltpu
from jax.sharding import PartitionSpec as P

SEG = 512
LANE = 128
GROUP = 8


def chirp_matrix(chirp_phase):
    tap_count = chirp_phase.shape[0]
    tap_scale = 1.0 / jnp.sqrt(jnp.float32(tap_count))
    real_taps = jnp.cos(chirp_phase) * tap_scale
    imag_taps = jnp.sin(chirp_phase) * tap_scale

    def banded(values):
        padded = jnp.concatenate([values, jnp.zeros((tap_count + 1,), jnp.float32)])
        return (
            jnp.tile(padded, tap_count)[: 2 * tap_count * tap_count]
            .reshape(tap_count, 2 * tap_count)
            .T
        )

    real_band = banded(real_taps)[: tap_count + LANE, :LANE]
    imag_band = banded(imag_taps)[: tap_count + LANE, :LANE]
    upper = jnp.concatenate([real_band, -imag_band], axis=1)
    lower = jnp.concatenate([imag_band, real_band], axis=1)
    return jnp.concatenate([upper, lower], axis=0).astype(jnp.bfloat16)


def compress_chunks(echo_full, filter_matrix, chunk_total):
    pulses, planes, bin_count = echo_full.shape
    taps = filter_matrix.shape[0] // planes - LANE
    reach = taps // LANE
    padded = jnp.pad(
        echo_full, ((0, 0), (0, 0), (0, (chunk_total + reach) * LANE - bin_count))
    )
    chunks = padded.reshape(pulses, planes, chunk_total + reach, LANE)
    windows = jnp.concatenate(
        [chunks[:, :, lead : lead + chunk_total] for lead in range(reach + 1)], axis=3
    )
    windows = windows.transpose(0, 2, 1, 3).reshape(pulses * chunk_total, -1)
    filtered = jnp.dot(windows, filter_matrix, preferred_element_type=jnp.float32)
    filtered = lax.reduce_precision(filtered, 8, 7)
    return filtered.reshape(pulses, chunk_total, planes * LANE)


def records_kernel(
    starts_ref, owner_ref, row_ref, coef_ref, prof_ref, out_ref, counts, *, capacity, out_rows
):
    slots = starts_ref.shape[0]
    owners = counts.shape[0]
    per_owner = capacity + 1
    lane_ids = lax.broadcasted_iota(jnp.int32, (GROUP, LANE), 1)
    row_ids = lax.broadcasted_iota(jnp.int32, (GROUP, LANE), 0)
    flat_ids = row_ids * LANE + lane_ids
    out_ref[...] = jnp.zeros(out_ref.shape, out_ref.dtype)

    def clear(o, carry):
        counts[o] = 0
        return carry

    lax.fori_loop(0, owners, clear, 0)

    def record(j, carry):
        owner = jnp.clip(owner_ref[j], 0, owners - 1)
        rank = jnp.minimum(counts[owner], capacity - 1)
        counts[owner] = rank + 1
        info_slot = owner * per_owner + capacity
        mark = rank * out_rows + jnp.clip(row_ref[j], 0, out_rows - 1)
        out_ref[info_slot] = jnp.where(flat_ids == mark, 1.0, out_ref[info_slot]).astype(out_ref.dtype)
        st = starts_ref[j]
        first = st // LANE
        off = st - first * LANE
        aligned = pl.multiple_of((first // GROUP) * GROUP, GROUP)
        lift = (2 * GROUP - (first - aligned)) % (2 * GROUP)
        parts = []
        for k in range(2):
            rows = prof_ref[k, pl.ds(aligned, 2 * GROUP), :]
            rows = pltpu.roll(rows, lift, 0)[:GROUP]
            parts.append((rows[:, :LANE], rows[:, LANE:]))
        (re0, im0), (re1, im1) = parts
        c0, s0, c1, s1, sc = (coef_ref[i, j] for i in range(5))
        out_re = ((c0 * re0 + c1 * re1) - (s0 * im0 + s1 * im1)) * sc
        out_im = ((c0 * im0 + c1 * im1) + (s0 * re0 + s1 * re1)) * sc
        turn = (LANE - off) % LANE
        keep = lane_ids < LANE - off
        shifted = []
        for z in (out_re, out_im):
            rot = pltpu.roll(z, turn, 1)
            shifted.append(jnp.where(keep, rot, pltpu.roll(rot, GROUP - 1, 0)))
        tile = jnp.where(
            row_ids < GROUP // 2, shifted[0], pltpu.roll(shifted[1], GROUP // 2, 0)
        )
        out_ref[owner * per_owner + rank] = tile.astype(out_ref.dtype)
        return carry

    lax.fori_loop(0, slots, record, 0, unroll=8)


def form_payload(prof, starts, owners, dest_rows, coef, owner_total, capacity, out_rows):
    vmem = pl.BlockSpec(memory_space=pltpu.VMEM)
    smem = pl.BlockSpec(memory_space=pltpu.SMEM)
    kernel = functools.partial(records_kernel, capacity=capacity, out_rows=out_rows)
    return pl.pallas_call(
        kernel,
        out_shape=jax.ShapeDtypeStruct(
            (owner_total * (capacity + 1), GROUP, LANE), jnp.bfloat16
        ),
        in_specs=[smem, smem, smem, smem, vmem],
        out_specs=vmem,
        scratch_shapes=[pltpu.SMEM((owner_total,), jnp.int32)],
    )(starts, owners, dest_rows, coef, prof)


def on_device(
    echo,
    chirp_phase,
    rec_phase,
    rec_start,
    rec_owner,
    rec_row,
    rec_weight,
    rec_count,
    prior,
    interp_weight,
):
    pulse_count = lax.axis_size("pulse")
    range_count = lax.axis_size("range")
    owner_total = pulse_count * range_count
    axes = ("pulse", "range")

    slot_count = rec_start.shape[1]
    owners = rec_owner[0, :, 0]
    dest_rows = rec_row[0]
    out_rows = interp_weight.shape[0]
    capacity = max(2, 3 * slot_count // (2 * owner_total))
    per_owner = capacity + 1
    slot_total = owner_total * per_owner

    filter_matrix = chirp_matrix(chirp_phase)
    if range_count == 2:
        other = lax.ppermute(echo, "range", [(0, 1), (1, 0)])
        first = lax.axis_index("range") == 0
        raw_echo = jnp.where(
            first, jnp.concatenate([echo, other], axis=2), jnp.concatenate([other, echo], axis=2)
        )
    else:
        raw_echo = lax.all_gather(echo, "range", axis=2, tiled=True)
    pulses, planes, bin_total = raw_echo.shape
    chunk_total = bin_total // LANE + 2 * GROUP
    prof = compress_chunks(raw_echo, filter_matrix, chunk_total)

    starts = rec_start[0]
    phases = rec_phase[0]
    weights = rec_weight[0]
    live_mask = (jnp.arange(slot_count) < rec_count[0, 0]).astype(jnp.float32)
    scales = live_mask * weights / jnp.sqrt(jnp.float32(pulses))
    turns = phases.T
    cosine = lax.reduce_precision(jnp.cos(turns), 8, 7)
    sine_part = lax.reduce_precision(jnp.sin(turns), 8, 7)
    coef = jnp.stack([cosine[0], sine_part[0], cosine[1], sine_part[1], scales])

    outgoing = form_payload(
        prof, starts, owners, dest_rows, coef, owner_total, capacity, out_rows
    )
    incoming = lax.all_to_all(
        outgoing.reshape(owner_total, per_owner, GROUP, LANE), axes, 0, 0, tiled=True
    )
    data = incoming[:, :capacity]
    row_table = incoming[:, capacity].reshape(owner_total, GROUP * LANE)[
        :, : capacity * out_rows
    ].reshape(owner_total, capacity, out_rows)
    gathered = jnp.einsum(
        "dkr,dkql->rql", row_table, data, preferred_element_type=jnp.float32
    )
    gathered = gathered.reshape(out_rows, planes, -1)
    fine = jnp.einsum(
        "rm,mps->rps", interp_weight, prior, preferred_element_type=jnp.float32
    )
    return fine + gathered


def solution(mesh):
    placed = (
        P("pulse", None, "range"),
        P(),
        P("range", "pulse", None),
        P("range", "pulse"),
        P("range", "pulse", None),
        P("range", "pulse"),
        P("range", "pulse"),
        P("range", "pulse"),
        P("pulse", None, "range"),
        P(),
    )
    return jax.shard_map(
        on_device, mesh=mesh, in_specs=placed, out_specs=P("pulse", None, "range"), check_vma=False
    )
```

```python
import functools

import jax
import jax.numpy as jnp
from jax import lax
from jax.experimental import pallas as pl
from jax.experimental.pallas import tpu as pltpu
from jax.sharding import PartitionSpec as P

SEG = 512
LANE = 128
GROUP = 8


def chirp_matrix(chirp_phase):
    tap_count = chirp_phase.shape[0]
    tap_scale = 1.0 / jnp.sqrt(jnp.float32(tap_count))
    real_taps = jnp.cos(chirp_phase) * tap_scale
    imag_taps = jnp.sin(chirp_phase) * tap_scale

    def banded(values):
        padded = jnp.concatenate([values, jnp.zeros((tap_count + 1,), jnp.float32)])
        return (
            jnp.tile(padded, tap_count)[: 2 * tap_count * tap_count]
            .reshape(tap_count, 2 * tap_count)
            .T
        )

    real_band = banded(real_taps)[: tap_count + LANE, :LANE]
    imag_band = banded(imag_taps)[: tap_count + LANE, :LANE]
    upper = jnp.concatenate([real_band, -imag_band], axis=1)
    lower = jnp.concatenate([imag_band, real_band], axis=1)
    return jnp.concatenate([upper, lower], axis=0).astype(jnp.bfloat16)


def compress_chunks(echo_full, filter_matrix, chunk_total):
    pulses, planes, bin_count = echo_full.shape
    taps = filter_matrix.shape[0] // planes - LANE
    reach = taps // LANE
    padded = jnp.pad(
        echo_full, ((0, 0), (0, 0), (0, (chunk_total + reach) * LANE - bin_count))
    )
    chunks = padded.reshape(pulses, planes, chunk_total + reach, LANE)
    windows = jnp.concatenate(
        [chunks[:, :, lead : lead + chunk_total] for lead in range(reach + 1)], axis=3
    )
    windows = windows.transpose(0, 2, 1, 3).reshape(pulses * chunk_total, -1)
    filtered = jnp.dot(windows, filter_matrix, preferred_element_type=jnp.float32)
    filtered = lax.reduce_precision(filtered, 8, 7)
    return filtered.reshape(pulses, chunk_total, planes * LANE)


def records_kernel(
    starts_ref, owner_ref, row_ref, coef_ref, echo_ref, filter_ref, out_ref, counts, prof_ref,
    *, capacity, out_rows
):
    pulses, planes, _, _ = echo_ref.shape
    chunk_total = prof_ref.shape[1]
    reach = filter_ref.shape[0] // (planes * LANE)
    for k in range(pulses):
        acc = jnp.zeros((chunk_total, planes * LANE), jnp.float32)
        for p in range(planes):
            for lead in range(reach):
                piece = echo_ref[k, p, lead : lead + chunk_total, :]
                band = filter_ref[(p * reach + lead) * LANE : (p * reach + lead + 1) * LANE, :]
                acc = acc + jnp.dot(piece, band, preferred_element_type=jnp.float32)
        prof_ref[k] = acc.astype(jnp.bfloat16).astype(jnp.float32)
    slots = starts_ref.shape[0]
    owners = counts.shape[0]
    per_owner = capacity + 1
    lane_ids = lax.broadcasted_iota(jnp.int32, (GROUP, LANE), 1)
    row_ids = lax.broadcasted_iota(jnp.int32, (GROUP, LANE), 0)
    flat_ids = row_ids * LANE + lane_ids
    out_ref[...] = jnp.zeros(out_ref.shape, out_ref.dtype)

    def clear(o, carry):
        counts[o] = 0
        return carry

    lax.fori_loop(0, owners, clear, 0)

    def record(j, carry):
        owner = jnp.clip(owner_ref[j], 0, owners - 1)
        rank = jnp.minimum(counts[owner], capacity - 1)
        counts[owner] = rank + 1
        info_slot = owner * per_owner + capacity
        mark = rank * out_rows + jnp.clip(row_ref[j], 0, out_rows - 1)
        out_ref[info_slot] = jnp.where(flat_ids == mark, 1.0, out_ref[info_slot]).astype(out_ref.dtype)
        st = starts_ref[j]
        first = st // LANE
        off = st - first * LANE
        aligned = pl.multiple_of((first // GROUP) * GROUP, GROUP)
        lift = (2 * GROUP - (first - aligned)) % (2 * GROUP)
        parts = []
        for k in range(2):
            rows = prof_ref[k, pl.ds(aligned, 2 * GROUP), :]
            rows = pltpu.roll(rows, lift, 0)[:GROUP]
            parts.append((rows[:, :LANE], rows[:, LANE:]))
        (re0, im0), (re1, im1) = parts
        c0, s0, c1, s1, sc = (coef_ref[i, j] for i in range(5))
        out_re = ((c0 * re0 + c1 * re1) - (s0 * im0 + s1 * im1)) * sc
        out_im = ((c0 * im0 + c1 * im1) + (s0 * re0 + s1 * re1)) * sc
        turn = (LANE - off) % LANE
        keep = lane_ids < LANE - off
        shifted = []
        for z in (out_re, out_im):
            rot = pltpu.roll(z, turn, 1)
            shifted.append(jnp.where(keep, rot, pltpu.roll(rot, GROUP - 1, 0)))
        tile = jnp.where(
            row_ids < GROUP // 2, shifted[0], pltpu.roll(shifted[1], GROUP // 2, 0)
        )
        out_ref[owner * per_owner + rank] = tile.astype(out_ref.dtype)
        return carry

    lax.fori_loop(0, slots, record, 0, unroll=8)


def form_payload(echo_chunks, filter_matrix, chunk_total, starts, owners, dest_rows, coef, owner_total, capacity, out_rows):
    vmem = pl.BlockSpec(memory_space=pltpu.VMEM)
    smem = pl.BlockSpec(memory_space=pltpu.SMEM)
    kernel = functools.partial(records_kernel, capacity=capacity, out_rows=out_rows)
    return pl.pallas_call(
        kernel,
        out_shape=jax.ShapeDtypeStruct(
            (owner_total * (capacity + 1), GROUP, LANE), jnp.bfloat16
        ),
        in_specs=[smem, smem, smem, smem, vmem, vmem],
        out_specs=vmem,
        scratch_shapes=[
            pltpu.SMEM((owner_total,), jnp.int32),
            pltpu.VMEM((echo_chunks.shape[0], chunk_total, 2 * LANE), jnp.float32),
        ],
    )(starts, owners, dest_rows, coef, echo_chunks, filter_matrix)


def on_device(
    echo,
    chirp_phase,
    rec_phase,
    rec_start,
    rec_owner,
    rec_row,
    rec_weight,
    rec_count,
    prior,
    interp_weight,
):
    pulse_count = lax.axis_size("pulse")
    range_count = lax.axis_size("range")
    owner_total = pulse_count * range_count
    axes = ("pulse", "range")

    slot_count = rec_start.shape[1]
    owners = rec_owner[0, :, 0]
    dest_rows = rec_row[0]
    out_rows = interp_weight.shape[0]
    capacity = max(2, 3 * slot_count // (2 * owner_total))
    per_owner = capacity + 1
    slot_total = owner_total * per_owner

    filter_matrix = chirp_matrix(chirp_phase)
    if range_count == 2:
        other = lax.ppermute(echo, "range", [(0, 1), (1, 0)])
        first = lax.axis_index("range") == 0
        raw_echo = jnp.where(
            first, jnp.concatenate([echo, other], axis=2), jnp.concatenate([other, echo], axis=2)
        )
    else:
        raw_echo = lax.all_gather(echo, "range", axis=2, tiled=True)
    pulses, planes, bin_total = raw_echo.shape
    chunk_total = bin_total // LANE + 2 * GROUP
    reach = filter_matrix.shape[0] // (planes * LANE)
    echo_chunks = jnp.pad(
        raw_echo, ((0, 0), (0, 0), (0, (chunk_total + reach) * LANE - bin_total))
    ).reshape(pulses, planes, chunk_total + reach, LANE)

    starts = rec_start[0]
    phases = rec_phase[0]
    weights = rec_weight[0]
    live_mask = (jnp.arange(slot_count) < rec_count[0, 0]).astype(jnp.float32)
    scales = live_mask * weights / jnp.sqrt(jnp.float32(pulses))
    turns = phases.T
    cosine = lax.reduce_precision(jnp.cos(turns), 8, 7)
    sine_part = lax.reduce_precision(jnp.sin(turns), 8, 7)
    coef = jnp.stack([cosine[0], sine_part[0], cosine[1], sine_part[1], scales])

    outgoing = form_payload(
        echo_chunks, filter_matrix, chunk_total, starts, owners, dest_rows, coef,
        owner_total, capacity, out_rows,
    )
    incoming = lax.all_to_all(
        outgoing.reshape(owner_total, per_owner, GROUP, LANE), axes, 0, 0, tiled=True
    )
    data = incoming[:, :capacity]
    row_table = incoming[:, capacity].reshape(owner_total, GROUP * LANE)[
        :, : capacity * out_rows
    ].reshape(owner_total, capacity, out_rows)
    gathered = jnp.einsum(
        "dkr,dkql->rql", row_table, data, preferred_element_type=jnp.float32
    )
    gathered = gathered.reshape(out_rows, planes, -1)
    fine = jnp.einsum(
        "rm,mps->rps", interp_weight, prior, preferred_element_type=jnp.float32
    )
    return fine + gathered


def solution(mesh):
    placed = (
        P("pulse", None, "range"),
        P(),
        P("range", "pulse", None),
        P("range", "pulse"),
        P("range", "pulse", None),
        P("range", "pulse"),
        P("range", "pulse"),
        P("range", "pulse"),
        P("pulse", None, "range"),
        P(),
    )
    return jax.shard_map(
        on_device, mesh=mesh, in_specs=placed, out_specs=P("pulse", None, "range"), check_vma=False
    )
```

```python
import functools

import jax
import jax.numpy as jnp
from jax import lax
from jax.experimental import pallas as pl
from jax.experimental.pallas import tpu as pltpu
from jax.sharding import PartitionSpec as P

SEG = 512
LANE = 128
GROUP = 8


def setup_kernel(chirp_ref, turns_ref, scale_ref, filter_ref, coef_ref):
    taps = chirp_ref.shape[1]
    rows = filter_ref.shape[0] // 2
    span = filter_ref.shape[1] // 2
    phase = chirp_ref[...]
    tap_scale = 1.0 / jnp.sqrt(jnp.float32(taps))
    bands = []
    for wave in (jnp.cos(phase) * tap_scale, jnp.sin(phase) * tap_scale):
        row = jnp.concatenate([wave, jnp.zeros((1, span - taps), jnp.float32)], axis=1)
        spread = jnp.broadcast_to(row, (rows, span))
        bands.append(pltpu.roll(spread, 0, 1, stride=1, stride_axis=0))
    real_band, imag_band = bands
    filter_ref[0:rows, 0:span] = real_band.astype(filter_ref.dtype)
    filter_ref[0:rows, span : 2 * span] = imag_band.astype(filter_ref.dtype)
    filter_ref[rows : 2 * rows, 0:span] = (-imag_band).astype(filter_ref.dtype)
    filter_ref[rows : 2 * rows, span : 2 * span] = real_band.astype(filter_ref.dtype)
    turns = turns_ref[...]
    cosine = jnp.cos(turns).astype(jnp.bfloat16).astype(jnp.float32)
    sine_part = jnp.sin(turns).astype(jnp.bfloat16).astype(jnp.float32)
    coef_ref[...] = jnp.zeros(coef_ref.shape, coef_ref.dtype)
    coef_ref[0:1, :] = cosine[0:1]
    coef_ref[1:2, :] = sine_part[0:1]
    coef_ref[2:3, :] = cosine[1:2]
    coef_ref[3:4, :] = sine_part[1:2]
    coef_ref[4:5, :] = scale_ref[...]


def setup_tables(chirp_phase, turns, scales):
    taps = chirp_phase.shape[0]
    slots = turns.shape[1]
    vmem = pl.BlockSpec(memory_space=pltpu.VMEM)
    return pl.pallas_call(
        setup_kernel,
        out_shape=(
            jax.ShapeDtypeStruct((2 * LANE, 2 * (taps + LANE)), jnp.bfloat16),
            jax.ShapeDtypeStruct((GROUP, slots), jnp.float32),
        ),
        in_specs=[vmem, vmem, vmem],
        out_specs=(vmem, vmem),
    )(chirp_phase.reshape(1, taps), turns, scales.reshape(1, slots))


def compress_chunks(echo_full, filter_matrix, chunk_total):
    pulses, planes, bin_count = echo_full.shape
    taps = filter_matrix.shape[1] // planes - LANE
    reach = taps // LANE
    padded = jnp.pad(
        echo_full, ((0, 0), (0, 0), (0, (chunk_total + reach) * LANE - bin_count))
    )
    chunks = padded.reshape(pulses, planes, chunk_total + reach, LANE)
    windows = jnp.concatenate(
        [chunks[:, :, lead : lead + chunk_total] for lead in range(reach + 1)], axis=3
    )
    windows = windows.transpose(0, 2, 1, 3).reshape(pulses * chunk_total, -1)
    filtered = lax.dot_general(
        windows, filter_matrix, (((1,), (1,)), ((), ())), preferred_element_type=jnp.float32
    )
    filtered = lax.reduce_precision(filtered, 8, 7)
    return filtered.reshape(pulses, chunk_total, planes * LANE)


def records_kernel(
    starts_ref, owner_ref, row_ref, coef_ref, prof_ref, out_ref, counts, *, capacity, out_rows
):
    slots = starts_ref.shape[0]
    owners = counts.shape[0]
    per_owner = capacity + 1
    lane_ids = lax.broadcasted_iota(jnp.int32, (GROUP, LANE), 1)
    row_ids = lax.broadcasted_iota(jnp.int32, (GROUP, LANE), 0)
    flat_ids = row_ids * LANE + lane_ids
    out_ref[...] = jnp.zeros(out_ref.shape, out_ref.dtype)

    def clear(o, carry):
        counts[o] = 0
        return carry

    lax.fori_loop(0, owners, clear, 0)

    def record(j, carry):
        owner = jnp.clip(owner_ref[j], 0, owners - 1)
        rank = jnp.minimum(counts[owner], capacity - 1)
        counts[owner] = rank + 1
        info_slot = owner * per_owner + capacity
        mark = rank * out_rows + jnp.clip(row_ref[j], 0, out_rows - 1)
        out_ref[info_slot] = jnp.where(flat_ids == mark, 1.0, out_ref[info_slot]).astype(out_ref.dtype)
        st = starts_ref[j]
        first = st // LANE
        off = st - first * LANE
        aligned = pl.multiple_of((first // GROUP) * GROUP, GROUP)
        lift = (2 * GROUP - (first - aligned)) % (2 * GROUP)
        parts = []
        for k in range(2):
            rows = prof_ref[k, pl.ds(aligned, 2 * GROUP), :]
            rows = pltpu.roll(rows, lift, 0)[:GROUP]
            parts.append((rows[:, :LANE], rows[:, LANE:]))
        (re0, im0), (re1, im1) = parts
        c0, s0, c1, s1, sc = (coef_ref[i, j] for i in range(5))
        out_re = ((c0 * re0 + c1 * re1) - (s0 * im0 + s1 * im1)) * sc
        out_im = ((c0 * im0 + c1 * im1) + (s0 * re0 + s1 * re1)) * sc
        turn = (LANE - off) % LANE
        keep = lane_ids < LANE - off
        shifted = []
        for z in (out_re, out_im):
            rot = pltpu.roll(z, turn, 1)
            shifted.append(jnp.where(keep, rot, pltpu.roll(rot, GROUP - 1, 0)))
        tile = jnp.where(
            row_ids < GROUP // 2, shifted[0], pltpu.roll(shifted[1], GROUP // 2, 0)
        )
        out_ref[owner * per_owner + rank] = tile.astype(out_ref.dtype)
        return carry

    lax.fori_loop(0, slots, record, 0, unroll=8)


def form_payload(prof, starts, owners, dest_rows, coef, owner_total, capacity, out_rows):
    vmem = pl.BlockSpec(memory_space=pltpu.VMEM)
    smem = pl.BlockSpec(memory_space=pltpu.SMEM)
    kernel = functools.partial(records_kernel, capacity=capacity, out_rows=out_rows)
    return pl.pallas_call(
        kernel,
        out_shape=jax.ShapeDtypeStruct(
            (owner_total * (capacity + 1), GROUP, LANE), jnp.bfloat16
        ),
        in_specs=[smem, smem, smem, smem, vmem],
        out_specs=vmem,
        scratch_shapes=[pltpu.SMEM((owner_total,), jnp.int32)],
    )(starts, owners, dest_rows, coef, prof)


def on_device(
    echo,
    chirp_phase,
    rec_phase,
    rec_start,
    rec_owner,
    rec_row,
    rec_weight,
    rec_count,
    prior,
    interp_weight,
):
    pulse_count = lax.axis_size("pulse")
    range_count = lax.axis_size("range")
    owner_total = pulse_count * range_count
    axes = ("pulse", "range")

    slot_count = rec_start.shape[1]
    owners = rec_owner[0, :, 0]
    dest_rows = rec_row[0]
    out_rows = interp_weight.shape[0]
    capacity = max(2, 3 * slot_count // (2 * owner_total))
    per_owner = capacity + 1
    slot_total = owner_total * per_owner

    if range_count == 2:
        other = lax.ppermute(echo, "range", [(0, 1), (1, 0)])
        first = lax.axis_index("range") == 0
        raw_echo = jnp.where(
            first, jnp.concatenate([echo, other], axis=2), jnp.concatenate([other, echo], axis=2)
        )
    else:
        raw_echo = lax.all_gather(echo, "range", axis=2, tiled=True)
    pulses, planes, bin_total = raw_echo.shape
    chunk_total = bin_total // LANE + 2 * GROUP

    starts = rec_start[0]
    phases = rec_phase[0]
    weights = rec_weight[0]
    live_mask = (jnp.arange(slot_count) < rec_count[0, 0]).astype(jnp.float32)
    scales = live_mask * weights / jnp.sqrt(jnp.float32(pulses))
    filter_matrix, coef = setup_tables(chirp_phase, phases.T, scales)
    prof = compress_chunks(raw_echo, filter_matrix, chunk_total)

    outgoing = form_payload(
        prof, starts, owners, dest_rows, coef, owner_total, capacity, out_rows
    )
    incoming = lax.all_to_all(
        outgoing.reshape(owner_total, per_owner, GROUP, LANE), axes, 0, 0, tiled=True
    )
    data = incoming[:, :capacity]
    row_table = incoming[:, capacity].reshape(owner_total, GROUP * LANE)[
        :, : capacity * out_rows
    ].reshape(owner_total, capacity, out_rows)
    gathered = jnp.einsum(
        "dkr,dkql->rql", row_table, data, preferred_element_type=jnp.float32
    )
    gathered = gathered.reshape(out_rows, planes, -1)
    fine = jnp.einsum(
        "rm,mps->rps", interp_weight, prior, preferred_element_type=jnp.float32
    )
    return fine + gathered


def solution(mesh):
    placed = (
        P("pulse", None, "range"),
        P(),
        P("range", "pulse", None),
        P("range", "pulse"),
        P("range", "pulse", None),
        P("range", "pulse"),
        P("range", "pulse"),
        P("range", "pulse"),
        P("pulse", None, "range"),
        P(),
    )
    return jax.shard_map(
        on_device, mesh=mesh, in_specs=placed, out_specs=P("pulse", None, "range"), check_vma=False
    )
```

```python
import functools

import jax
import jax.numpy as jnp
from jax import lax
from jax.experimental import pallas as pl
from jax.experimental.pallas import tpu as pltpu
from jax.sharding import PartitionSpec as P

SEG = 512
LANE = 128
GROUP = 8


def chirp_matrix(chirp_phase):
    tap_count = chirp_phase.shape[0]
    tap_scale = 1.0 / jnp.sqrt(jnp.float32(tap_count))
    real_taps = jnp.cos(chirp_phase) * tap_scale
    imag_taps = jnp.sin(chirp_phase) * tap_scale

    def banded(values):
        padded = jnp.concatenate([values, jnp.zeros((tap_count + 1,), jnp.float32)])
        return (
            jnp.tile(padded, tap_count)[: 2 * tap_count * tap_count]
            .reshape(tap_count, 2 * tap_count)
            .T
        )

    real_band = banded(real_taps)[: tap_count + LANE, :LANE]
    imag_band = banded(imag_taps)[: tap_count + LANE, :LANE]
    upper = jnp.concatenate([real_band, -imag_band], axis=1)
    lower = jnp.concatenate([imag_band, real_band], axis=1)
    return jnp.concatenate([upper, lower], axis=0).astype(jnp.bfloat16)


def compress_chunks(echo_full, filter_matrix, chunk_total):
    pulses, planes, bin_count = echo_full.shape
    taps = filter_matrix.shape[0] // planes - LANE
    reach = taps // LANE
    padded = jnp.pad(
        echo_full, ((0, 0), (0, 0), (0, (chunk_total + reach) * LANE - bin_count))
    )
    chunks = padded.reshape(pulses, planes, chunk_total + reach, LANE)
    windows = jnp.concatenate(
        [chunks[:, :, lead : lead + chunk_total] for lead in range(reach + 1)], axis=3
    )
    windows = windows.transpose(0, 2, 1, 3).reshape(pulses * chunk_total, -1)
    filtered = jnp.dot(windows, filter_matrix, preferred_element_type=jnp.float32)
    filtered = lax.reduce_precision(filtered, 8, 7)
    return filtered.reshape(pulses, chunk_total, planes * LANE)


def records_kernel(
    starts_ref, owner_ref, row_ref, coef_ref, prof_ref, out_ref, counts, *, capacity, out_rows
):
    slots = starts_ref.shape[0]
    owners = counts.shape[0]
    per_owner = capacity
    lane_ids = lax.broadcasted_iota(jnp.int32, (GROUP, LANE), 1)
    row_ids = lax.broadcasted_iota(jnp.int32, (GROUP, LANE), 0)
    out_ref[...] = jnp.zeros(out_ref.shape, out_ref.dtype)

    def clear(o, carry):
        counts[o] = 0
        return carry

    lax.fori_loop(0, owners, clear, 0)

    def record(j, carry):
        owner = jnp.clip(owner_ref[j], 0, owners - 1)
        rank = jnp.minimum(counts[owner], capacity - 1)
        counts[owner] = rank + 1
        st = starts_ref[j]
        first = st // LANE
        off = st - first * LANE
        aligned = pl.multiple_of((first // GROUP) * GROUP, GROUP)
        lift = (2 * GROUP - (first - aligned)) % (2 * GROUP)
        parts = []
        for k in range(2):
            rows = prof_ref[k, pl.ds(aligned, 2 * GROUP), :]
            rows = pltpu.roll(rows, lift, 0)[:GROUP]
            parts.append((rows[:, :LANE], rows[:, LANE:]))
        (re0, im0), (re1, im1) = parts
        c0, s0, c1, s1, sc = (coef_ref[i, j] for i in range(5))
        out_re = ((c0 * re0 + c1 * re1) - (s0 * im0 + s1 * im1)) * sc
        out_im = ((c0 * im0 + c1 * im1) + (s0 * re0 + s1 * re1)) * sc
        turn = (LANE - off) % LANE
        keep = lane_ids < LANE - off
        shifted = []
        for z in (out_re, out_im):
            rot = pltpu.roll(z, turn, 1)
            shifted.append(jnp.where(keep, rot, pltpu.roll(rot, GROUP - 1, 0)))
        tile = jnp.where(
            row_ids < GROUP // 2, shifted[0], pltpu.roll(shifted[1], GROUP // 2, 0)
        )
        out_ref[owner * per_owner + rank] = tile.astype(out_ref.dtype)
        return carry

    lax.fori_loop(0, slots, record, 0, unroll=8)


def form_payload(prof, starts, owners, dest_rows, coef, owner_total, capacity, out_rows):
    vmem = pl.BlockSpec(memory_space=pltpu.VMEM)
    smem = pl.BlockSpec(memory_space=pltpu.SMEM)
    kernel = functools.partial(records_kernel, capacity=capacity, out_rows=out_rows)
    return pl.pallas_call(
        kernel,
        out_shape=jax.ShapeDtypeStruct(
            (owner_total * capacity, GROUP, LANE), jnp.bfloat16
        ),
        in_specs=[smem, smem, smem, smem, vmem],
        out_specs=vmem,
        scratch_shapes=[pltpu.SMEM((owner_total,), jnp.int32)],
    )(starts, owners, dest_rows, coef, prof)


def on_device(
    echo,
    chirp_phase,
    rec_phase,
    rec_start,
    rec_owner,
    rec_row,
    rec_weight,
    rec_count,
    prior,
    interp_weight,
):
    pulse_count = lax.axis_size("pulse")
    range_count = lax.axis_size("range")
    owner_total = pulse_count * range_count
    axes = ("pulse", "range")

    slot_count = rec_start.shape[1]
    owners = rec_owner[0, :, 0]
    dest_rows = rec_row[0]
    out_rows = interp_weight.shape[0]
    capacity = max(2, 3 * slot_count // (2 * owner_total))
    per_owner = capacity
    codes = (owners * out_rows + dest_rows).astype(jnp.float32)
    all_codes = lax.all_gather(codes, axes, axis=0, tiled=False)
    all_codes, echo = lax.optimization_barrier((all_codes, echo))
    all_codes = all_codes.astype(jnp.int32)

    filter_matrix = chirp_matrix(chirp_phase)
    if range_count == 2:
        other = lax.ppermute(echo, "range", [(0, 1), (1, 0)])
        first = lax.axis_index("range") == 0
        raw_echo = jnp.where(
            first, jnp.concatenate([echo, other], axis=2), jnp.concatenate([other, echo], axis=2)
        )
    else:
        raw_echo = lax.all_gather(echo, "range", axis=2, tiled=True)
    pulses, planes, bin_total = raw_echo.shape
    chunk_total = bin_total // LANE + 2 * GROUP
    prof = compress_chunks(raw_echo, filter_matrix, chunk_total)

    starts = rec_start[0]
    phases = rec_phase[0]
    weights = rec_weight[0]
    live_mask = (jnp.arange(slot_count) < rec_count[0, 0]).astype(jnp.float32)
    scales = live_mask * weights / jnp.sqrt(jnp.float32(pulses))
    turns = phases.T
    cosine = lax.reduce_precision(jnp.cos(turns), 8, 7)
    sine_part = lax.reduce_precision(jnp.sin(turns), 8, 7)
    coef = jnp.stack([cosine[0], sine_part[0], cosine[1], sine_part[1], scales])

    outgoing = form_payload(
        prof, starts, owners, dest_rows, coef, owner_total, capacity, out_rows
    )
    incoming = lax.all_to_all(
        outgoing.reshape(owner_total, per_owner, GROUP, LANE), axes, 0, 0, tiled=True
    )
    data = incoming
    me = lax.axis_index("pulse") * range_count + lax.axis_index("range")
    mine = (all_codes // out_rows == me).astype(jnp.int32)
    rank = jnp.cumsum(mine, axis=1) - mine
    picks = (mine[:, None, :] == 1) & (rank[:, None, :] == jnp.arange(capacity)[None, :, None])
    slot_rows = jnp.sum(jnp.where(picks, (all_codes % out_rows)[:, None, :], 0), axis=2)
    taken = jnp.any(picks, axis=2)
    row_table = (
        taken[:, :, None] & (slot_rows[:, :, None] == jnp.arange(out_rows)[None, None, :])
    ).astype(jnp.bfloat16)
    gathered = jnp.einsum(
        "dkr,dkql->rql", row_table, data, preferred_element_type=jnp.float32
    )
    gathered = gathered.reshape(out_rows, planes, -1)
    fine = jnp.einsum(
        "rm,mps->rps", interp_weight, prior, preferred_element_type=jnp.float32
    )
    return fine + gathered


def solution(mesh):
    placed = (
        P("pulse", None, "range"),
        P(),
        P("range", "pulse", None),
        P("range", "pulse"),
        P("range", "pulse", None),
        P("range", "pulse"),
        P("range", "pulse"),
        P("range", "pulse"),
        P("pulse", None, "range"),
        P(),
    )
    return jax.shard_map(
        on_device, mesh=mesh, in_specs=placed, out_specs=P("pulse", None, "range"), check_vma=False
    )
```

```python
import functools

import jax
import jax.numpy as jnp
from jax import lax
from jax.experimental import pallas as pl
from jax.experimental.pallas import tpu as pltpu
from jax.sharding import PartitionSpec as P

SEG = 512
LANE = 128
GROUP = 8


def chirp_matrix(chirp_phase):
    tap_count = chirp_phase.shape[0]
    tap_scale = 1.0 / jnp.sqrt(jnp.float32(tap_count))
    real_taps = jnp.cos(chirp_phase) * tap_scale
    imag_taps = jnp.sin(chirp_phase) * tap_scale

    def banded(values):
        padded = jnp.concatenate([values, jnp.zeros((tap_count + 1,), jnp.float32)])
        return (
            jnp.tile(padded, tap_count)[: 2 * tap_count * tap_count]
            .reshape(tap_count, 2 * tap_count)
            .T
        )

    real_band = banded(real_taps)[: tap_count + LANE, :LANE]
    imag_band = banded(imag_taps)[: tap_count + LANE, :LANE]
    upper = jnp.concatenate([real_band, -imag_band], axis=1)
    lower = jnp.concatenate([imag_band, real_band], axis=1)
    return jnp.concatenate([upper, lower], axis=0).astype(jnp.bfloat16)


def compress_chunks(echo_full, filter_matrix, chunk_total):
    pulses, planes, bin_count = echo_full.shape
    taps = filter_matrix.shape[0] // planes - LANE
    reach = taps // LANE
    padded = jnp.pad(
        echo_full, ((0, 0), (0, 0), (0, (chunk_total + reach) * LANE - bin_count))
    )
    chunks = padded.reshape(pulses, planes, chunk_total + reach, LANE)
    windows = jnp.concatenate(
        [chunks[:, :, lead : lead + chunk_total] for lead in range(reach + 1)], axis=3
    )
    windows = windows.transpose(0, 2, 1, 3).reshape(pulses * chunk_total, -1)
    filtered = jnp.dot(windows, filter_matrix, preferred_element_type=jnp.float32)
    filtered = lax.reduce_precision(filtered, 8, 7)
    return filtered.reshape(pulses, chunk_total, planes * LANE)


def records_kernel(
    starts_ref, owner_ref, row_ref, coef_ref, prof_ref, out_ref, counts, *, capacity, out_rows
):
    slots = starts_ref.shape[0]
    owners = counts.shape[0]
    per_owner = capacity + 1
    lane_ids = lax.broadcasted_iota(jnp.int32, (GROUP, LANE), 1)
    row_ids = lax.broadcasted_iota(jnp.int32, (GROUP, LANE), 0)
    flat_ids = row_ids * LANE + lane_ids
    out_ref[...] = jnp.zeros(out_ref.shape, out_ref.dtype)

    def clear(o, carry):
        counts[o] = 0
        return carry

    lax.fori_loop(0, owners, clear, 0)

    def record(j, carry):
        owner = jnp.minimum(owner_ref[j], owners - 1)
        rank = jnp.minimum(counts[owner], capacity - 1)
        counts[owner] = rank + 1
        base_slot = owner * per_owner
        info_slot = base_slot + capacity
        mark = rank * out_rows + (row_ref[j] & (out_rows - 1))
        out_ref[info_slot] = jnp.where(flat_ids == mark, 1.0, out_ref[info_slot]).astype(out_ref.dtype)
        st = starts_ref[j]
        first = lax.shift_right_logical(st, 7)
        off = st & (LANE - 1)
        aligned = pl.multiple_of(first & -GROUP, GROUP)
        lift = (2 * GROUP - (first & (GROUP - 1))) & (2 * GROUP - 1)
        parts = []
        for k in range(2):
            rows = prof_ref[k, pl.ds(aligned, 2 * GROUP), :]
            rows = pltpu.roll(rows, lift, 0)[:GROUP]
            parts.append((rows[:, :LANE], rows[:, LANE:]))
        (re0, im0), (re1, im1) = parts
        c0, s0, c1, s1, sc = (coef_ref[i, j] for i in range(5))
        out_re = ((c0 * re0 + c1 * re1) - (s0 * im0 + s1 * im1)) * sc
        out_im = ((c0 * im0 + c1 * im1) + (s0 * re0 + s1 * re1)) * sc
        turn = (LANE - off) & (LANE - 1)
        keep = lane_ids < LANE - off
        shifted = []
        for z in (out_re, out_im):
            rot = pltpu.roll(z, turn, 1)
            shifted.append(jnp.where(keep, rot, pltpu.roll(rot, GROUP - 1, 0)))
        tile = jnp.where(
            row_ids < GROUP // 2, shifted[0], pltpu.roll(shifted[1], GROUP // 2, 0)
        )
        out_ref[base_slot + rank] = tile.astype(out_ref.dtype)
        return carry

    lax.fori_loop(0, slots, record, 0, unroll=8)


def form_payload(prof, starts, owners, dest_rows, coef, owner_total, capacity, out_rows):
    vmem = pl.BlockSpec(memory_space=pltpu.VMEM)
    smem = pl.BlockSpec(memory_space=pltpu.SMEM)
    kernel = functools.partial(records_kernel, capacity=capacity, out_rows=out_rows)
    return pl.pallas_call(
        kernel,
        out_shape=jax.ShapeDtypeStruct(
            (owner_total * (capacity + 1), GROUP, LANE), jnp.bfloat16
        ),
        in_specs=[smem, smem, smem, smem, vmem],
        out_specs=vmem,
        scratch_shapes=[pltpu.SMEM((owner_total,), jnp.int32)],
    )(starts, owners, dest_rows, coef, prof)


def on_device(
    echo,
    chirp_phase,
    rec_phase,
    rec_start,
    rec_owner,
    rec_row,
    rec_weight,
    rec_count,
    prior,
    interp_weight,
):
    pulse_count = lax.axis_size("pulse")
    range_count = lax.axis_size("range")
    owner_total = pulse_count * range_count
    axes = ("pulse", "range")

    slot_count = rec_start.shape[1]
    owners = rec_owner[0, :, 0]
    dest_rows = rec_row[0]
    out_rows = interp_weight.shape[0]
    capacity = max(2, 3 * slot_count // (2 * owner_total))
    per_owner = capacity + 1
    slot_total = owner_total * per_owner

    filter_matrix = chirp_matrix(chirp_phase)
    if range_count == 2:
        other = lax.ppermute(echo, "range", [(0, 1), (1, 0)])
        first = lax.axis_index("range") == 0
        raw_echo = jnp.where(
            first, jnp.concatenate([echo, other], axis=2), jnp.concatenate([other, echo], axis=2)
        )
    else:
        raw_echo = lax.all_gather(echo, "range", axis=2, tiled=True)
    pulses, planes, bin_total = raw_echo.shape
    chunk_total = bin_total // LANE + 2 * GROUP
    prof = compress_chunks(raw_echo, filter_matrix, chunk_total)

    starts = rec_start[0]
    phases = rec_phase[0]
    weights = rec_weight[0]
    live_mask = (jnp.arange(slot_count) < rec_count[0, 0]).astype(jnp.float32)
    scales = live_mask * weights / jnp.sqrt(jnp.float32(pulses))
    turns = phases.T
    cosine = lax.reduce_precision(jnp.cos(turns), 8, 7)
    sine_part = lax.reduce_precision(jnp.sin(turns), 8, 7)
    coef = jnp.stack([cosine[0], sine_part[0], cosine[1], sine_part[1], scales])

    outgoing = form_payload(
        prof, starts, owners, dest_rows, coef, owner_total, capacity, out_rows
    )
    incoming = lax.all_to_all(
        outgoing.reshape(owner_total, per_owner, GROUP, LANE), axes, 0, 0, tiled=True
    )
    data = incoming[:, :capacity]
    row_table = incoming[:, capacity].reshape(owner_total, GROUP * LANE)[
        :, : capacity * out_rows
    ].reshape(owner_total, capacity, out_rows)
    gathered = jnp.einsum(
        "dkr,dkql->rql", row_table, data, preferred_element_type=jnp.float32
    )
    gathered = gathered.reshape(out_rows, planes, -1)
    fine = jnp.einsum(
        "rm,mps->rps", interp_weight, prior, preferred_element_type=jnp.float32
    )
    return fine + gathered


def solution(mesh):
    placed = (
        P("pulse", None, "range"),
        P(),
        P("range", "pulse", None),
        P("range", "pulse"),
        P("range", "pulse", None),
        P("range", "pulse"),
        P("range", "pulse"),
        P("range", "pulse"),
        P("pulse", None, "range"),
        P(),
    )
    return jax.shard_map(
        on_device, mesh=mesh, in_specs=placed, out_specs=P("pulse", None, "range"), check_vma=False
    )
```

```python
import functools

import jax
import jax.numpy as jnp
from jax import lax
from jax.experimental import pallas as pl
from jax.experimental.pallas import tpu as pltpu
from jax.sharding import PartitionSpec as P

SEG = 512
LANE = 128
GROUP = 8


def chirp_matrix(chirp_phase):
    tap_count = chirp_phase.shape[0]
    tap_scale = 1.0 / jnp.sqrt(jnp.float32(tap_count))
    real_taps = jnp.cos(chirp_phase) * tap_scale
    imag_taps = jnp.sin(chirp_phase) * tap_scale

    def banded(values):
        padded = jnp.concatenate([values, jnp.zeros((tap_count + 1,), jnp.float32)])
        return (
            jnp.tile(padded, tap_count)[: 2 * tap_count * tap_count]
            .reshape(tap_count, 2 * tap_count)
            .T
        )

    real_band = banded(real_taps)[: tap_count + LANE, :LANE]
    imag_band = banded(imag_taps)[: tap_count + LANE, :LANE]
    upper = jnp.concatenate([real_band, -imag_band], axis=1)
    lower = jnp.concatenate([imag_band, real_band], axis=1)
    return jnp.concatenate([upper, lower], axis=0).astype(jnp.bfloat16)


def compress_chunks(echo_full, filter_matrix, chunk_total):
    pulses, planes, bin_count = echo_full.shape
    taps = filter_matrix.shape[0] // planes - LANE
    reach = taps // LANE
    padded = jnp.pad(
        echo_full, ((0, 0), (0, 0), (0, (chunk_total + reach) * LANE - bin_count))
    )
    chunks = padded.reshape(pulses, planes, chunk_total + reach, LANE)
    windows = jnp.concatenate(
        [chunks[:, :, lead : lead + chunk_total] for lead in range(reach + 1)], axis=3
    )
    windows = windows.transpose(0, 2, 1, 3).reshape(pulses * chunk_total, -1)
    filtered = jnp.dot(windows, filter_matrix, preferred_element_type=jnp.float32)
    filtered = lax.reduce_precision(filtered, 8, 7)
    return filtered.reshape(pulses, chunk_total, planes * LANE)


def records_kernel(
    starts_ref, owner_ref, row_ref, coef_ref, prof_ref, out_ref, counts, *, capacity, out_rows
):
    slots = starts_ref.shape[0]
    owners = counts.shape[0]
    per_owner = capacity + 1
    lane_ids = lax.broadcasted_iota(jnp.int32, (GROUP, LANE), 1)
    row_ids = lax.broadcasted_iota(jnp.int32, (GROUP, LANE), 0)
    flat_ids = row_ids * LANE + lane_ids
    out_ref[...] = jnp.zeros(out_ref.shape, out_ref.dtype)

    def clear(o, carry):
        counts[o] = 0
        return carry

    lax.fori_loop(0, owners, clear, 0)

    def record(j, carry):
        owner = jnp.minimum(owner_ref[j], owners - 1)
        rank = jnp.minimum(counts[owner], capacity - 1)
        counts[owner] = rank + 1
        base_slot = owner * per_owner
        info_slot = base_slot + capacity
        mark = rank * out_rows + (row_ref[j] & (out_rows - 1))
        out_ref[info_slot] = jnp.where(flat_ids == mark, 1.0, out_ref[info_slot]).astype(out_ref.dtype)
        st = starts_ref[j]
        first = lax.shift_right_logical(st, 7)
        off = st & (LANE - 1)
        aligned = pl.multiple_of(first & -GROUP, GROUP)
        lift = (2 * GROUP - (first & (GROUP - 1))) & (2 * GROUP - 1)
        parts = []
        for k in range(2):
            rows = prof_ref[k, pl.ds(aligned, 2 * GROUP), :]
            rows = pltpu.roll(rows, lift, 0)[:GROUP]
            parts.append((rows[:, :LANE], rows[:, LANE:]))
        (re0, im0), (re1, im1) = parts
        c0, s0, c1, s1, sc = (coef_ref[i, j] for i in range(5))
        out_re = ((c0 * re0 + c1 * re1) - (s0 * im0 + s1 * im1)) * sc
        out_im = ((c0 * im0 + c1 * im1) + (s0 * re0 + s1 * re1)) * sc
        turn = (LANE - off) & (LANE - 1)
        keep = lane_ids < LANE - off
        shifted = []
        for z in (out_re, out_im):
            rot = pltpu.roll(z, turn, 1)
            shifted.append(jnp.where(keep, rot, pltpu.roll(rot, GROUP - 1, 0)))
        tile = jnp.where(
            row_ids < GROUP // 2, shifted[0], pltpu.roll(shifted[1], GROUP // 2, 0)
        )
        out_ref[base_slot + rank] = tile.astype(out_ref.dtype)
        return carry

    lax.fori_loop(0, slots, record, 0, unroll=16)


def form_payload(prof, starts, owners, dest_rows, coef, owner_total, capacity, out_rows):
    vmem = pl.BlockSpec(memory_space=pltpu.VMEM)
    smem = pl.BlockSpec(memory_space=pltpu.SMEM)
    kernel = functools.partial(records_kernel, capacity=capacity, out_rows=out_rows)
    return pl.pallas_call(
        kernel,
        out_shape=jax.ShapeDtypeStruct(
            (owner_total * (capacity + 1), GROUP, LANE), jnp.bfloat16
        ),
        in_specs=[smem, smem, smem, smem, vmem],
        out_specs=vmem,
        scratch_shapes=[pltpu.SMEM((owner_total,), jnp.int32)],
    )(starts, owners, dest_rows, coef, prof)


def on_device(
    echo,
    chirp_phase,
    rec_phase,
    rec_start,
    rec_owner,
    rec_row,
    rec_weight,
    rec_count,
    prior,
    interp_weight,
):
    pulse_count = lax.axis_size("pulse")
    range_count = lax.axis_size("range")
    owner_total = pulse_count * range_count
    axes = ("pulse", "range")

    slot_count = rec_start.shape[1]
    owners = rec_owner[0, :, 0]
    dest_rows = rec_row[0]
    out_rows = interp_weight.shape[0]
    capacity = max(2, 3 * slot_count // (2 * owner_total))
    per_owner = capacity + 1
    slot_total = owner_total * per_owner

    filter_matrix = chirp_matrix(chirp_phase)
    if range_count == 2:
        other = lax.ppermute(echo, "range", [(0, 1), (1, 0)])
        first = lax.axis_index("range") == 0
        raw_echo = jnp.where(
            first, jnp.concatenate([echo, other], axis=2), jnp.concatenate([other, echo], axis=2)
        )
    else:
        raw_echo = lax.all_gather(echo, "range", axis=2, tiled=True)
    pulses, planes, bin_total = raw_echo.shape
    chunk_total = bin_total // LANE + 2 * GROUP
    prof = compress_chunks(raw_echo, filter_matrix, chunk_total)

    starts = rec_start[0]
    phases = rec_phase[0]
    weights = rec_weight[0]
    live_mask = (jnp.arange(slot_count) < rec_count[0, 0]).astype(jnp.float32)
    scales = live_mask * weights / jnp.sqrt(jnp.float32(pulses))
    turns = phases.T
    cosine = lax.reduce_precision(jnp.cos(turns), 8, 7)
    sine_part = lax.reduce_precision(jnp.sin(turns), 8, 7)
    coef = jnp.stack([cosine[0], sine_part[0], cosine[1], sine_part[1], scales])

    outgoing = form_payload(
        prof, starts, owners, dest_rows, coef, owner_total, capacity, out_rows
    )
    incoming = lax.all_to_all(
        outgoing.reshape(owner_total, per_owner, GROUP, LANE), axes, 0, 0, tiled=True
    )
    data = incoming[:, :capacity]
    row_table = incoming[:, capacity].reshape(owner_total, GROUP * LANE)[
        :, : capacity * out_rows
    ].reshape(owner_total, capacity, out_rows)
    gathered = jnp.einsum(
        "dkr,dkql->rql", row_table, data, preferred_element_type=jnp.float32
    )
    gathered = gathered.reshape(out_rows, planes, -1)
    fine = jnp.einsum(
        "rm,mps->rps", interp_weight, prior, preferred_element_type=jnp.float32
    )
    return fine + gathered


def solution(mesh):
    placed = (
        P("pulse", None, "range"),
        P(),
        P("range", "pulse", None),
        P("range", "pulse"),
        P("range", "pulse", None),
        P("range", "pulse"),
        P("range", "pulse"),
        P("range", "pulse"),
        P("pulse", None, "range"),
        P(),
    )
    return jax.shard_map(
        on_device, mesh=mesh, in_specs=placed, out_specs=P("pulse", None, "range"), check_vma=False
    )
```

```python
import functools

import jax
import jax.numpy as jnp
from jax import lax
from jax.experimental import pallas as pl
from jax.experimental.pallas import tpu as pltpu
from jax.sharding import PartitionSpec as P

SEG = 512
LANE = 128
GROUP = 8


def chirp_matrix(chirp_phase):
    tap_count = chirp_phase.shape[0]
    tap_scale = 1.0 / jnp.sqrt(jnp.float32(tap_count))
    real_taps = jnp.cos(chirp_phase) * tap_scale
    imag_taps = jnp.sin(chirp_phase) * tap_scale

    def banded(values):
        padded = jnp.concatenate([values, jnp.zeros((tap_count + 1,), jnp.float32)])
        return (
            jnp.tile(padded, tap_count)[: 2 * tap_count * tap_count]
            .reshape(tap_count, 2 * tap_count)
            .T
        )

    real_band = banded(real_taps)[: tap_count + LANE, :LANE]
    imag_band = banded(imag_taps)[: tap_count + LANE, :LANE]
    upper = jnp.concatenate([real_band, -imag_band], axis=1)
    lower = jnp.concatenate([imag_band, real_band], axis=1)
    return jnp.concatenate([upper, lower], axis=0).astype(jnp.bfloat16)


def compress_chunks(echo_full, filter_matrix, chunk_total):
    pulses, planes, bin_count = echo_full.shape
    taps = filter_matrix.shape[0] // planes - LANE
    reach = taps // LANE
    padded = jnp.pad(
        echo_full, ((0, 0), (0, 0), (0, (chunk_total + reach) * LANE - bin_count))
    )
    chunks = padded.reshape(pulses, planes, chunk_total + reach, LANE)
    windows = jnp.concatenate(
        [chunks[:, :, lead : lead + chunk_total] for lead in range(reach + 1)], axis=3
    )
    windows = windows.transpose(0, 2, 1, 3).reshape(pulses * chunk_total, -1)
    filtered = jnp.dot(windows, filter_matrix, preferred_element_type=jnp.float32)
    filtered = lax.reduce_precision(filtered, 8, 7)
    return filtered.reshape(pulses, chunk_total, planes * LANE)


def records_kernel(
    starts_ref, owner_ref, row_ref, coef_ref, prof_ref, out_ref, counts, *, capacity, out_rows
):
    slots = starts_ref.shape[0]
    owners = counts.shape[0]
    per_owner = capacity + 1
    lane_ids = lax.broadcasted_iota(jnp.int32, (GROUP, LANE), 1)
    row_ids = lax.broadcasted_iota(jnp.int32, (GROUP, LANE), 0)
    flat_ids = row_ids * LANE + lane_ids
    out_ref[...] = jnp.zeros(out_ref.shape, out_ref.dtype)

    def clear(o, carry):
        counts[o] = 0
        return carry

    lax.fori_loop(0, owners, clear, 0)

    def record(j, carry):
        owner = jnp.minimum(owner_ref[j], owners - 1)
        rank = jnp.minimum(counts[owner], capacity - 1)
        counts[owner] = rank + 1
        base_slot = owner * per_owner
        info_slot = base_slot + capacity
        mark = rank * out_rows + (row_ref[j] & (out_rows - 1))
        out_ref[info_slot] = jnp.where(flat_ids == mark, 1.0, out_ref[info_slot]).astype(out_ref.dtype)
        st = starts_ref[j]
        first = lax.shift_right_logical(st, 7)
        off = st & (LANE - 1)
        aligned = pl.multiple_of(first & -GROUP, GROUP)
        lift = (2 * GROUP - (first & (GROUP - 1))) & (2 * GROUP - 1)
        parts = []
        for k in range(2):
            rows = prof_ref[k, pl.ds(aligned, 2 * GROUP), :]
            rows = pltpu.roll(rows, lift, 0)[:GROUP]
            parts.append((rows[:, :LANE], rows[:, LANE:]))
        (re0, im0), (re1, im1) = parts
        c0, s0, c1, s1, sc = (coef_ref[i, j] for i in range(5))
        out_re = ((c0 * re0 + c1 * re1) - (s0 * im0 + s1 * im1)) * sc
        out_im = ((c0 * im0 + c1 * im1) + (s0 * re0 + s1 * re1)) * sc
        turn = (LANE - off) & (LANE - 1)
        keep = lane_ids < LANE - off
        shifted = []
        for z in (out_re, out_im):
            rot = pltpu.roll(z, turn, 1)
            shifted.append(jnp.where(keep, rot, pltpu.roll(rot, GROUP - 1, 0)))
        tile = jnp.where(
            row_ids < GROUP // 2, shifted[0], pltpu.roll(shifted[1], GROUP // 2, 0)
        )
        out_ref[base_slot + rank] = tile.astype(out_ref.dtype)
        return carry

    lax.fori_loop(0, slots, record, 0, unroll=16)


def form_payload(prof, starts, owners, dest_rows, coef, owner_total, capacity, out_rows):
    vmem = pl.BlockSpec(memory_space=pltpu.VMEM)
    smem = pl.BlockSpec(memory_space=pltpu.SMEM)
    kernel = functools.partial(records_kernel, capacity=capacity, out_rows=out_rows)
    return pl.pallas_call(
        kernel,
        out_shape=jax.ShapeDtypeStruct(
            (owner_total * (capacity + 1), GROUP, LANE), jnp.bfloat16
        ),
        in_specs=[smem, smem, smem, smem, vmem],
        out_specs=vmem,
        scratch_shapes=[pltpu.SMEM((owner_total,), jnp.int32)],
    )(starts, owners, dest_rows, coef, prof)


def on_device(
    echo,
    chirp_phase,
    rec_phase,
    rec_start,
    rec_owner,
    rec_row,
    rec_weight,
    rec_count,
    prior,
    interp_weight,
):
    pulse_count = lax.axis_size("pulse")
    range_count = lax.axis_size("range")
    owner_total = pulse_count * range_count
    axes = ("pulse", "range")

    slot_count = rec_start.shape[1]
    owners = rec_owner[0, :, 0]
    dest_rows = rec_row[0]
    out_rows = interp_weight.shape[0]
    capacity = max(2, 3 * slot_count // (2 * owner_total))
    per_owner = capacity + 1
    slot_total = owner_total * per_owner

    filter_matrix = chirp_matrix(chirp_phase)
    if range_count == 2:
        other = lax.ppermute(echo, "range", [(0, 1), (1, 0)])
        first = lax.axis_index("range") == 0
        raw_echo = jnp.concatenate(
            [jnp.where(first, echo, other), jnp.where(first, other, echo)], axis=2
        )
    else:
        raw_echo = lax.all_gather(echo, "range", axis=2, tiled=True)
    pulses, planes, bin_total = raw_echo.shape
    chunk_total = bin_total // LANE + 2 * GROUP
    prof = compress_chunks(raw_echo, filter_matrix, chunk_total)

    starts = rec_start[0]
    phases = rec_phase[0]
    weights = rec_weight[0]
    live_mask = (jnp.arange(slot_count) < rec_count[0, 0]).astype(jnp.float32)
    scales = live_mask * weights / jnp.sqrt(jnp.float32(pulses))
    turns = phases.T
    cosine = lax.reduce_precision(jnp.cos(turns), 8, 7)
    sine_part = lax.reduce_precision(jnp.sin(turns), 8, 7)
    coef = jnp.stack([cosine[0], sine_part[0], cosine[1], sine_part[1], scales])

    outgoing = form_payload(
        prof, starts, owners, dest_rows, coef, owner_total, capacity, out_rows
    )
    incoming = lax.all_to_all(
        outgoing.reshape(owner_total, per_owner, GROUP, LANE), axes, 0, 0, tiled=True
    )
    data = incoming[:, :capacity]
    row_table = incoming[:, capacity].reshape(owner_total, GROUP * LANE)[
        :, : capacity * out_rows
    ].reshape(owner_total, capacity, out_rows)
    gathered = jnp.einsum(
        "dkr,dkql->rql", row_table, data, preferred_element_type=jnp.float32
    )
    gathered = gathered.reshape(out_rows, planes, -1)
    fine = jnp.einsum(
        "rm,mps->rps", interp_weight, prior, preferred_element_type=jnp.float32
    )
    return fine + gathered


def solution(mesh):
    placed = (
        P("pulse", None, "range"),
        P(),
        P("range", "pulse", None),
        P("range", "pulse"),
        P("range", "pulse", None),
        P("range", "pulse"),
        P("range", "pulse"),
        P("range", "pulse"),
        P("pulse", None, "range"),
        P(),
    )
    return jax.shard_map(
        on_device, mesh=mesh, in_specs=placed, out_specs=P("pulse", None, "range"), check_vma=False
    )
```

```python
import functools

import jax
import jax.numpy as jnp
from jax import lax
from jax.experimental import pallas as pl
from jax.experimental.pallas import tpu as pltpu
from jax.sharding import PartitionSpec as P

SEG = 512
LANE = 128
GROUP = 8


def chirp_matrix(chirp_phase):
    tap_count = chirp_phase.shape[0]
    tap_scale = 1.0 / jnp.sqrt(jnp.float32(tap_count))
    real_taps = jnp.cos(chirp_phase) * tap_scale
    imag_taps = jnp.sin(chirp_phase) * tap_scale

    def banded(values):
        padded = jnp.concatenate([values, jnp.zeros((tap_count + 1,), jnp.float32)])
        return (
            jnp.tile(padded, tap_count)[: 2 * tap_count * tap_count]
            .reshape(tap_count, 2 * tap_count)
            .T
        )

    real_band = banded(real_taps)[: tap_count + LANE, :LANE]
    imag_band = banded(imag_taps)[: tap_count + LANE, :LANE]
    upper = jnp.concatenate([real_band, -imag_band], axis=1)
    lower = jnp.concatenate([imag_band, real_band], axis=1)
    return jnp.concatenate([upper, lower], axis=0).astype(jnp.bfloat16)


def compress_chunks(echo_full, filter_matrix, chunk_total):
    pulses, planes, bin_count = echo_full.shape
    taps = filter_matrix.shape[0] // planes - LANE
    reach = taps // LANE
    padded = jnp.pad(
        echo_full, ((0, 0), (0, 0), (0, (chunk_total + reach) * LANE - bin_count))
    )
    chunks = padded.reshape(pulses, planes, chunk_total + reach, LANE)
    windows = jnp.concatenate(
        [chunks[:, :, lead : lead + chunk_total] for lead in range(reach + 1)], axis=3
    )
    windows = windows.transpose(0, 2, 1, 3).reshape(pulses * chunk_total, -1)
    filtered = jnp.dot(windows, filter_matrix, preferred_element_type=jnp.float32)
    filtered = lax.reduce_precision(filtered, 8, 7)
    return filtered.reshape(pulses, chunk_total, planes * LANE)


def records_kernel(
    starts_ref, owner_ref, row_ref, coef_ref, prof_ref, out_ref, counts, *, capacity, out_rows
):
    slots = starts_ref.shape[0]
    owners = counts.shape[0]
    per_owner = capacity + 1
    lane_ids = lax.broadcasted_iota(jnp.int32, (GROUP, LANE), 1)
    row_ids = lax.broadcasted_iota(jnp.int32, (GROUP, LANE), 0)
    flat_ids = row_ids * LANE + lane_ids
    out_ref[...] = jnp.zeros(out_ref.shape, out_ref.dtype)

    def clear(o, carry):
        counts[o] = 0
        return carry

    lax.fori_loop(0, owners, clear, 0)

    def record(j, carry):
        owner = jnp.minimum(owner_ref[j], owners - 1)
        rank = jnp.minimum(counts[owner], capacity - 1)
        counts[owner] = rank + 1
        base_slot = owner * per_owner
        info_slot = base_slot + capacity
        mark = rank * out_rows + (row_ref[j] & (out_rows - 1))
        out_ref[info_slot] = jnp.where(flat_ids == mark, 1.0, out_ref[info_slot]).astype(out_ref.dtype)
        st = starts_ref[j]
        first = lax.shift_right_logical(st, 7)
        off = st & (LANE - 1)
        aligned = pl.multiple_of(first & -GROUP, GROUP)
        lift = (2 * GROUP - (first & (GROUP - 1))) & (2 * GROUP - 1)
        parts = []
        for k in range(2):
            rows = prof_ref[k, pl.ds(aligned, 2 * GROUP), :]
            rows = pltpu.roll(rows, lift, 0)[:GROUP]
            parts.append((rows[:, :LANE], rows[:, LANE:]))
        (re0, im0), (re1, im1) = parts
        c0, s0, c1, s1 = (coef_ref[i, j] for i in range(4))
        out_re = (c0 * re0 + c1 * re1) - (s0 * im0 + s1 * im1)
        out_im = (c0 * im0 + c1 * im1) + (s0 * re0 + s1 * re1)
        turn = (LANE - off) & (LANE - 1)
        keep = lane_ids < LANE - off
        shifted = []
        for z in (out_re, out_im):
            rot = pltpu.roll(z, turn, 1)
            shifted.append(jnp.where(keep, rot, pltpu.roll(rot, GROUP - 1, 0)))
        tile = jnp.where(
            row_ids < GROUP // 2, shifted[0], pltpu.roll(shifted[1], GROUP // 2, 0)
        )
        out_ref[base_slot + rank] = tile.astype(out_ref.dtype)
        return carry

    lax.fori_loop(0, slots, record, 0, unroll=16)


def form_payload(prof, starts, owners, dest_rows, coef, owner_total, capacity, out_rows):
    vmem = pl.BlockSpec(memory_space=pltpu.VMEM)
    smem = pl.BlockSpec(memory_space=pltpu.SMEM)
    kernel = functools.partial(records_kernel, capacity=capacity, out_rows=out_rows)
    return pl.pallas_call(
        kernel,
        out_shape=jax.ShapeDtypeStruct(
            (owner_total * (capacity + 1), GROUP, LANE), jnp.bfloat16
        ),
        in_specs=[smem, smem, smem, smem, vmem],
        out_specs=vmem,
        scratch_shapes=[pltpu.SMEM((owner_total,), jnp.int32)],
    )(starts, owners, dest_rows, coef, prof)


def on_device(
    echo,
    chirp_phase,
    rec_phase,
    rec_start,
    rec_owner,
    rec_row,
    rec_weight,
    rec_count,
    prior,
    interp_weight,
):
    pulse_count = lax.axis_size("pulse")
    range_count = lax.axis_size("range")
    owner_total = pulse_count * range_count
    axes = ("pulse", "range")

    slot_count = rec_start.shape[1]
    owners = rec_owner[0, :, 0]
    dest_rows = rec_row[0]
    out_rows = interp_weight.shape[0]
    capacity = max(2, 3 * slot_count // (2 * owner_total))
    per_owner = capacity + 1
    slot_total = owner_total * per_owner

    filter_matrix = chirp_matrix(chirp_phase)
    if range_count == 2:
        other = lax.ppermute(echo, "range", [(0, 1), (1, 0)])
        first = lax.axis_index("range") == 0
        raw_echo = jnp.concatenate(
            [jnp.where(first, echo, other), jnp.where(first, other, echo)], axis=2
        )
    else:
        raw_echo = lax.all_gather(echo, "range", axis=2, tiled=True)
    pulses, planes, bin_total = raw_echo.shape
    chunk_total = bin_total // LANE + 2 * GROUP
    prof = compress_chunks(raw_echo, filter_matrix, chunk_total)

    starts = rec_start[0]
    phases = rec_phase[0]
    weights = rec_weight[0]
    live_mask = (jnp.arange(slot_count) < rec_count[0, 0]).astype(jnp.float32)
    scales = live_mask * weights / jnp.sqrt(jnp.float32(pulses))
    turns = phases.T
    cosine = lax.reduce_precision(jnp.cos(turns), 8, 7)
    sine_part = lax.reduce_precision(jnp.sin(turns), 8, 7)
    coef = jnp.stack([cosine[0], sine_part[0], cosine[1], sine_part[1]]) * scales[None, :]

    outgoing = form_payload(
        prof, starts, owners, dest_rows, coef, owner_total, capacity, out_rows
    )
    incoming = lax.all_to_all(
        outgoing.reshape(owner_total, per_owner, GROUP, LANE), axes, 0, 0, tiled=True
    )
    data = incoming[:, :capacity]
    row_table = incoming[:, capacity].reshape(owner_total, GROUP * LANE)[
        :, : capacity * out_rows
    ].reshape(owner_total, capacity, out_rows)
    gathered = jnp.einsum(
        "dkr,dkql->rql", row_table, data, preferred_element_type=jnp.float32
    )
    gathered = gathered.reshape(out_rows, planes, -1)
    fine = jnp.einsum(
        "rm,mps->rps", interp_weight, prior, preferred_element_type=jnp.float32
    )
    return fine + gathered


def solution(mesh):
    placed = (
        P("pulse", None, "range"),
        P(),
        P("range", "pulse", None),
        P("range", "pulse"),
        P("range", "pulse", None),
        P("range", "pulse"),
        P("range", "pulse"),
        P("range", "pulse"),
        P("pulse", None, "range"),
        P(),
    )
    return jax.shard_map(
        on_device, mesh=mesh, in_specs=placed, out_specs=P("pulse", None, "range"), check_vma=False
    )
```

```python
import functools

import jax
import jax.numpy as jnp
from jax import lax
from jax.experimental import pallas as pl
from jax.experimental.pallas import tpu as pltpu
from jax.sharding import PartitionSpec as P

SEG = 512
LANE = 128
GROUP = 8


def chirp_matrix(chirp_phase):
    tap_count = chirp_phase.shape[0]
    tap_scale = 1.0 / jnp.sqrt(jnp.float32(tap_count))
    real_taps = jnp.cos(chirp_phase) * tap_scale
    imag_taps = jnp.sin(chirp_phase) * tap_scale

    def banded(values):
        padded = jnp.concatenate([values, jnp.zeros((tap_count + 1,), jnp.float32)])
        return (
            jnp.tile(padded, tap_count)[: 2 * tap_count * tap_count]
            .reshape(tap_count, 2 * tap_count)
            .T
        )

    real_band = banded(real_taps)[: tap_count + LANE, :LANE]
    imag_band = banded(imag_taps)[: tap_count + LANE, :LANE]
    upper = jnp.concatenate([real_band, -imag_band], axis=1)
    lower = jnp.concatenate([imag_band, real_band], axis=1)
    return jnp.concatenate([upper, lower], axis=0).astype(jnp.bfloat16)


def compress_chunks(echo_full, filter_matrix, chunk_total):
    pulses, planes, bin_count = echo_full.shape
    taps = filter_matrix.shape[0] // planes - LANE
    reach = taps // LANE
    padded = jnp.pad(
        echo_full, ((0, 0), (0, 0), (0, (chunk_total + reach) * LANE - bin_count))
    )
    chunks = padded.reshape(pulses, planes, chunk_total + reach, LANE)
    bands = filter_matrix.reshape(planes, reach + 1, LANE, -1)
    filtered = sum(
        jnp.einsum(
            "kpql,plo->kqo",
            chunks[:, :, lead : lead + chunk_total],
            bands[:, lead],
            preferred_element_type=jnp.float32,
        )
        for lead in range(reach + 1)
    )
    filtered = lax.reduce_precision(filtered, 8, 7)
    return filtered.reshape(pulses, chunk_total, planes * LANE)


def records_kernel(
    starts_ref, owner_ref, row_ref, coef_ref, prof_ref, out_ref, counts, *, capacity, out_rows
):
    slots = starts_ref.shape[0]
    owners = counts.shape[0]
    per_owner = capacity + 1
    lane_ids = lax.broadcasted_iota(jnp.int32, (GROUP, LANE), 1)
    row_ids = lax.broadcasted_iota(jnp.int32, (GROUP, LANE), 0)
    flat_ids = row_ids * LANE + lane_ids
    out_ref[...] = jnp.zeros(out_ref.shape, out_ref.dtype)

    def clear(o, carry):
        counts[o] = 0
        return carry

    lax.fori_loop(0, owners, clear, 0)

    def record(j, carry):
        owner = jnp.minimum(owner_ref[j], owners - 1)
        rank = jnp.minimum(counts[owner], capacity - 1)
        counts[owner] = rank + 1
        base_slot = owner * per_owner
        info_slot = base_slot + capacity
        mark = rank * out_rows + (row_ref[j] & (out_rows - 1))
        out_ref[info_slot] = jnp.where(flat_ids == mark, 1.0, out_ref[info_slot]).astype(out_ref.dtype)
        st = starts_ref[j]
        first = lax.shift_right_logical(st, 7)
        off = st & (LANE - 1)
        aligned = pl.multiple_of(first & -GROUP, GROUP)
        lift = (2 * GROUP - (first & (GROUP - 1))) & (2 * GROUP - 1)
        parts = []
        for k in range(2):
            rows = prof_ref[k, pl.ds(aligned, 2 * GROUP), :]
            rows = pltpu.roll(rows, lift, 0)[:GROUP]
            parts.append((rows[:, :LANE], rows[:, LANE:]))
        (re0, im0), (re1, im1) = parts
        c0, s0, c1, s1 = (coef_ref[i, j] for i in range(4))
        out_re = (c0 * re0 + c1 * re1) - (s0 * im0 + s1 * im1)
        out_im = (c0 * im0 + c1 * im1) + (s0 * re0 + s1 * re1)
        turn = (LANE - off) & (LANE - 1)
        keep = lane_ids < LANE - off
        shifted = []
        for z in (out_re, out_im):
            rot = pltpu.roll(z, turn, 1)
            shifted.append(jnp.where(keep, rot, pltpu.roll(rot, GROUP - 1, 0)))
        tile = jnp.where(
            row_ids < GROUP // 2, shifted[0], pltpu.roll(shifted[1], GROUP // 2, 0)
        )
        out_ref[base_slot + rank] = tile.astype(out_ref.dtype)
        return carry

    lax.fori_loop(0, slots, record, 0, unroll=16)


def form_payload(prof, starts, owners, dest_rows, coef, owner_total, capacity, out_rows):
    vmem = pl.BlockSpec(memory_space=pltpu.VMEM)
    smem = pl.BlockSpec(memory_space=pltpu.SMEM)
    kernel = functools.partial(records_kernel, capacity=capacity, out_rows=out_rows)
    return pl.pallas_call(
        kernel,
        out_shape=jax.ShapeDtypeStruct(
            (owner_total * (capacity + 1), GROUP, LANE), jnp.bfloat16
        ),
        in_specs=[smem, smem, smem, smem, vmem],
        out_specs=vmem,
        scratch_shapes=[pltpu.SMEM((owner_total,), jnp.int32)],
    )(starts, owners, dest_rows, coef, prof)


def on_device(
    echo,
    chirp_phase,
    rec_phase,
    rec_start,
    rec_owner,
    rec_row,
    rec_weight,
    rec_count,
    prior,
    interp_weight,
):
    pulse_count = lax.axis_size("pulse")
    range_count = lax.axis_size("range")
    owner_total = pulse_count * range_count
    axes = ("pulse", "range")

    slot_count = rec_start.shape[1]
    owners = rec_owner[0, :, 0]
    dest_rows = rec_row[0]
    out_rows = interp_weight.shape[0]
    capacity = max(2, 3 * slot_count // (2 * owner_total))
    per_owner = capacity + 1
    slot_total = owner_total * per_owner

    filter_matrix = chirp_matrix(chirp_phase)
    if range_count == 2:
        other = lax.ppermute(echo, "range", [(0, 1), (1, 0)])
        first = lax.axis_index("range") == 0
        raw_echo = jnp.concatenate(
            [jnp.where(first, echo, other), jnp.where(first, other, echo)], axis=2
        )
    else:
        raw_echo = lax.all_gather(echo, "range", axis=2, tiled=True)
    pulses, planes, bin_total = raw_echo.shape
    chunk_total = bin_total // LANE + 2 * GROUP
    prof = compress_chunks(raw_echo, filter_matrix, chunk_total)

    starts = rec_start[0]
    phases = rec_phase[0]
    weights = rec_weight[0]
    live_mask = (jnp.arange(slot_count) < rec_count[0, 0]).astype(jnp.float32)
    scales = live_mask * weights / jnp.sqrt(jnp.float32(pulses))
    turns = phases.T
    cosine = lax.reduce_precision(jnp.cos(turns), 8, 7)
    sine_part = lax.reduce_precision(jnp.sin(turns), 8, 7)
    coef = jnp.stack([cosine[0], sine_part[0], cosine[1], sine_part[1]]) * scales[None, :]

    outgoing = form_payload(
        prof, starts, owners, dest_rows, coef, owner_total, capacity, out_rows
    )
    incoming = lax.all_to_all(
        outgoing.reshape(owner_total, per_owner, GROUP, LANE), axes, 0, 0, tiled=True
    )
    data = incoming[:, :capacity]
    row_table = incoming[:, capacity].reshape(owner_total, GROUP * LANE)[
        :, : capacity * out_rows
    ].reshape(owner_total, capacity, out_rows)
    gathered = jnp.einsum(
        "dkr,dkql->rql", row_table, data, preferred_element_type=jnp.float32
    )
    gathered = gathered.reshape(out_rows, planes, -1)
    fine = jnp.einsum(
        "rm,mps->rps", interp_weight, prior, preferred_element_type=jnp.float32
    )
    return fine + gathered


def solution(mesh):
    placed = (
        P("pulse", None, "range"),
        P(),
        P("range", "pulse", None),
        P("range", "pulse"),
        P("range", "pulse", None),
        P("range", "pulse"),
        P("range", "pulse"),
        P("range", "pulse"),
        P("pulse", None, "range"),
        P(),
    )
    return jax.shard_map(
        on_device, mesh=mesh, in_specs=placed, out_specs=P("pulse", None, "range"), check_vma=False
    )
```

```python
import functools

import jax
import jax.numpy as jnp
from jax import lax
from jax.experimental import pallas as pl
from jax.experimental.pallas import tpu as pltpu
from jax.sharding import PartitionSpec as P

SEG = 512
LANE = 128
GROUP = 8


def chirp_matrix(chirp_phase):
    tap_count = chirp_phase.shape[0]
    tap_scale = 1.0 / jnp.sqrt(jnp.float32(tap_count))
    real_taps = jnp.cos(chirp_phase) * tap_scale
    imag_taps = jnp.sin(chirp_phase) * tap_scale

    def banded(values):
        padded = jnp.concatenate([values, jnp.zeros((tap_count + 1,), jnp.float32)])
        return (
            jnp.tile(padded, tap_count)[: 2 * tap_count * tap_count]
            .reshape(tap_count, 2 * tap_count)
            .T
        )

    real_band = banded(real_taps)[: tap_count + LANE, :LANE]
    imag_band = banded(imag_taps)[: tap_count + LANE, :LANE]
    upper = jnp.concatenate([real_band, -imag_band], axis=1)
    lower = jnp.concatenate([imag_band, real_band], axis=1)
    return jnp.concatenate([upper, lower], axis=0).astype(jnp.bfloat16)


def compress_chunks(echo_full, filter_matrix, chunk_total):
    pulses, planes, bin_count = echo_full.shape
    taps = filter_matrix.shape[0] // planes - LANE
    reach = taps // LANE
    padded = jnp.pad(
        echo_full, ((0, 0), (0, 0), (0, (chunk_total + reach) * LANE - bin_count))
    )
    chunks = padded.reshape(pulses, planes, chunk_total + reach, LANE)
    windows = jnp.concatenate(
        [chunks[:, :, lead : lead + chunk_total] for lead in range(reach + 1)], axis=3
    )
    windows = windows.transpose(0, 2, 1, 3).reshape(pulses * chunk_total, -1)
    filtered = jnp.dot(windows, filter_matrix, preferred_element_type=jnp.float32)
    filtered = lax.reduce_precision(filtered, 8, 7)
    return filtered.reshape(pulses, chunk_total, planes * LANE)


def records_kernel(
    starts_ref, owner_ref, row_ref, coef_ref, prof_ref, out_ref, counts, *, capacity, out_rows
):
    slots = starts_ref.shape[0]
    owners = counts.shape[0]
    per_owner = capacity + 1
    lane_ids = lax.broadcasted_iota(jnp.int32, (GROUP, LANE), 1)
    row_ids = lax.broadcasted_iota(jnp.int32, (GROUP, LANE), 0)
    flat_ids = row_ids * LANE + lane_ids
    out_ref[...] = jnp.zeros(out_ref.shape, out_ref.dtype)

    def clear(o, carry):
        counts[o] = 0
        return carry

    lax.fori_loop(0, owners, clear, 0)

    def record(j, carry):
        owner = jnp.minimum(owner_ref[j], owners - 1)
        rank = jnp.minimum(counts[owner], capacity - 1)
        counts[owner] = rank + 1
        base_slot = owner * per_owner
        info_slot = base_slot + capacity
        mark = rank * out_rows + (row_ref[j] & (out_rows - 1))
        out_ref[info_slot] = jnp.where(flat_ids == mark, 1.0, out_ref[info_slot]).astype(out_ref.dtype)
        st = starts_ref[j]
        first = lax.shift_right_logical(st, 7)
        off = st & (LANE - 1)
        aligned = pl.multiple_of(first & -GROUP, GROUP)
        lift = (2 * GROUP - (first & (GROUP - 1))) & (2 * GROUP - 1)
        parts = []
        for k in range(2):
            rows = prof_ref[k, pl.ds(aligned, 2 * GROUP), :]
            rows = pltpu.roll(rows, lift, 0)[:GROUP]
            parts.append((rows[:, :LANE], rows[:, LANE:]))
        (re0, im0), (re1, im1) = parts
        c0, s0, c1, s1 = (coef_ref[i, j] for i in range(4))
        out_re = (c0 * re0 + c1 * re1) - (s0 * im0 + s1 * im1)
        out_im = (c0 * im0 + c1 * im1) + (s0 * re0 + s1 * re1)
        turn = (LANE - off) & (LANE - 1)
        keep = lane_ids < LANE - off
        shifted = []
        for z in (out_re, out_im):
            rot = pltpu.roll(z, turn, 1)
            shifted.append(jnp.where(keep, rot, pltpu.roll(rot, GROUP - 1, 0)))
        tile = jnp.where(
            row_ids < GROUP // 2, shifted[0], pltpu.roll(shifted[1], GROUP // 2, 0)
        )
        out_ref[base_slot + rank] = tile.astype(out_ref.dtype)
        return carry

    lax.fori_loop(0, slots, record, 0, unroll=16)


def form_payload(prof, starts, owners, dest_rows, coef, owner_total, capacity, out_rows):
    vmem = pl.BlockSpec(memory_space=pltpu.VMEM)
    smem = pl.BlockSpec(memory_space=pltpu.SMEM)
    kernel = functools.partial(records_kernel, capacity=capacity, out_rows=out_rows)
    return pl.pallas_call(
        kernel,
        out_shape=jax.ShapeDtypeStruct(
            (owner_total * (capacity + 1), GROUP, LANE), jnp.bfloat16
        ),
        in_specs=[smem, smem, smem, smem, vmem],
        out_specs=vmem,
        scratch_shapes=[pltpu.SMEM((owner_total,), jnp.int32)],
    )(starts, owners, dest_rows, coef, prof)


def on_device(
    echo,
    chirp_phase,
    rec_phase,
    rec_start,
    rec_owner,
    rec_row,
    rec_weight,
    rec_count,
    prior,
    interp_weight,
):
    pulse_count = lax.axis_size("pulse")
    range_count = lax.axis_size("range")
    owner_total = pulse_count * range_count
    axes = ("pulse", "range")

    slot_count = rec_start.shape[1]
    owners = rec_owner[0, :, 0]
    dest_rows = rec_row[0]
    out_rows = interp_weight.shape[0]
    capacity = max(2, 3 * slot_count // (2 * owner_total))
    per_owner = capacity + 1
    slot_total = owner_total * per_owner

    filter_matrix = chirp_matrix(chirp_phase)
    if range_count == 2:
        other = lax.ppermute(echo, "range", [(0, 1), (1, 0)])
        first = lax.axis_index("range") == 0
        raw_echo = jnp.concatenate(
            [jnp.where(first, echo, other), jnp.where(first, other, echo)], axis=2
        )
    else:
        raw_echo = lax.all_gather(echo, "range", axis=2, tiled=True)
    pulses, planes, bin_total = raw_echo.shape
    chunk_total = bin_total // LANE + GROUP
    prof = compress_chunks(raw_echo, filter_matrix, chunk_total)

    starts = rec_start[0]
    phases = rec_phase[0]
    weights = rec_weight[0]
    live_mask = (jnp.arange(slot_count) < rec_count[0, 0]).astype(jnp.float32)
    scales = live_mask * weights / jnp.sqrt(jnp.float32(pulses))
    turns = phases.T
    cosine = lax.reduce_precision(jnp.cos(turns), 8, 7)
    sine_part = lax.reduce_precision(jnp.sin(turns), 8, 7)
    coef = jnp.stack([cosine[0], sine_part[0], cosine[1], sine_part[1]]) * scales[None, :]

    outgoing = form_payload(
        prof, starts, owners, dest_rows, coef, owner_total, capacity, out_rows
    )
    incoming = lax.all_to_all(
        outgoing.reshape(owner_total, per_owner, GROUP, LANE), axes, 0, 0, tiled=True
    )
    data = incoming[:, :capacity]
    row_table = incoming[:, capacity].reshape(owner_total, GROUP * LANE)[
        :, : capacity * out_rows
    ].reshape(owner_total, capacity, out_rows)
    gathered = jnp.einsum(
        "dkr,dkql->rql", row_table, data, preferred_element_type=jnp.float32
    )
    gathered = gathered.reshape(out_rows, planes, -1)
    fine = jnp.einsum(
        "rm,mps->rps", interp_weight, prior, preferred_element_type=jnp.float32
    )
    return fine + gathered


def solution(mesh):
    placed = (
        P("pulse", None, "range"),
        P(),
        P("range", "pulse", None),
        P("range", "pulse"),
        P("range", "pulse", None),
        P("range", "pulse"),
        P("range", "pulse"),
        P("range", "pulse"),
        P("pulse", None, "range"),
        P(),
    )
    return jax.shard_map(
        on_device, mesh=mesh, in_specs=placed, out_specs=P("pulse", None, "range"), check_vma=False
    )
```
